256 devices in a mesh: row: 32 (over x, y, core), col: 8 (over z).
Axes of the slice: x: 4, y: 4, z: 8, core: 2. Of those that a mesh axis runs over, the one named last changes fastest.
Arguments:
- matrix: float32 [16384, 16384], P('row', 'col'), may hold values from -9 to 9
- vectors: float32 [16384, 128], P('row'), may hold values from -0.125 to 0.125
- tfactor: float32 [128, 128], replicated, may hold values from -1 to 2, as said below
Outputs:
- updated: float32 [16384, 16384], P('row', 'col')
The draws below stay inside these ranges and needn't reach their ends.
Inputs may be any that keep to these rules, and one draw needn't show every extreme that they name: tfactor is upper triangular with its diagonal between 0.7 and 1.4.
All inputs are finite; a program needn't handle non-finite values.
Results may differ from the reference program's by a relative error of at most 0.000094.
Values sent between devices are 32-bit elements; how exact they have to be, the bound alone decides.
No kernel may reach another device: no remote copies, remote signals or barrier semaphores. Data moves between devices by JAX's collectives and lax.ppermute only.
A program may use at most 128 MiB of HBM per device.

```python
import math
import jax
import jax.numpy as jnp
from jax import lax

M = 16384
NB = 128


def draw_matrix(key, part):
    source = jax.random.truncated_normal(key, -6.0, 6.0, (M, M), jnp.float32)
    return ((source + source.T) * 0.7071).astype(jnp.float32)


def draw_tfactor(key, part):
    first, second = jax.random.split(jax.random.fold_in(key, 7))
    diagonal = jax.random.uniform(first, (NB,), jnp.float32, 0.7, 1.4)
    upper = jax.random.truncated_normal(second, -3.0, 3.0, (NB, NB), jnp.float32) * (0.35 / math.sqrt(NB))
    return (jnp.triu(upper, 1) + jnp.diag(diagonal)).astype(jnp.float32)


def level_of(rng, extent, shards, low, high):
    factor_of = 1.0
    for dim, parts in shards:
        heights = jax.random.uniform(jax.random.fold_in(jax.random.fold_in(rng, 6), dim), (parts,), jnp.float32, low / len(shards), high / len(shards))
        factor_of = factor_of * jnp.repeat(jnp.exp(heights), extent[dim] // parts).reshape((-1,) + (1,) * (len(extent) - 1 - dim))
    return factor_of


def noise(rng, dims, deviation, reach, pieces=(), held_as=jnp.bfloat16):
    drawn = deviation * jax.random.normal(rng, dims, jnp.float32)
    if pieces:
        drawn = drawn * level_of(rng, dims, pieces, -0.22, 0.18)
    return jnp.clip(drawn, -reach, reach).astype(held_as)


def setup_inputs(seed: int = 0) -> dict:
    key_list = jax.random.split(jax.random.key(seed), 4)
    return {
        "matrix": draw_matrix(jax.random.fold_in(key_list[3], 71), 0),
        "vectors": noise(key_list[1], (M, NB), (M // 8) ** -0.5, 0.125, ((0, 32),), jnp.float32),
        "tfactor": draw_tfactor(jax.random.fold_in(key_list[3], 71), 0),
    }


def mult(left, right):
    return jnp.dot(left, right, precision=lax.Precision.HIGHEST, preferred_element_type=jnp.float32)


def reference(matrix, vectors, tfactor):
    product_x = mult(matrix, vectors)
    product_y = mult(product_x, tfactor)
    cross = mult(vectors.T, product_y)
    coupling = mult(tfactor.T, cross)
    work = product_y - 0.5 * mult(vectors, coupling)
    rows_block = math.gcd(M, 1024)
    count_blocks = M // rows_block
    tiles = matrix.reshape(count_blocks, rows_block, M)
    vec_tiles = vectors.reshape(count_blocks, rows_block, NB)
    work_tiles = work.reshape(count_blocks, rows_block, NB)

    def update(items):
        tile, vec_tile, work_tile = items
        return tile - mult(vec_tile, work.T) - mult(work_tile, vectors.T)

    result = lax.map(update, (tiles, vec_tiles, work_tiles))
    return result.reshape(M, M)
```

```python
import jax
import jax.numpy as jnp
from jax import lax
from jax.sharding import PartitionSpec as P


def product(left, right):
    return jnp.dot(left, right, precision=lax.Precision.HIGHEST, preferred_element_type=jnp.float32)


def inner_product(left, right):
    return lax.dot_general(
        left,
        right,
        (((0,), (0,)), ((), ())),
        precision=lax.Precision.HIGHEST,
        preferred_element_type=jnp.float32,
    )


def butterfly_sum(value, axis, size):
    step = 1
    while step < size:
        pairs = [(i, i ^ step) for i in range(size)]
        value = value + lax.ppermute(value, axis, pairs)
        step *= 2
    return value


def to_columns(panel_rows):
    rows_here = panel_rows.shape[0]
    row_count = lax.axis_size("row")
    col_count = lax.axis_size("col")
    per = row_count // col_count
    row = lax.axis_index("row")
    gathered = jnp.zeros((per * rows_here,) + panel_rows.shape[1:], panel_rows.dtype)
    for j in range(per):
        pairs = []
        for src_row in range(row_count):
            for src_col in range(col_count):
                dst_row = per * src_col + (src_row % per + j) % per
                dst_col = src_row // per
                pairs.append((src_row * col_count + src_col, dst_row * col_count + dst_col))
        block = lax.ppermute(panel_rows, ("row", "col"), pairs)
        slot = (row % per - j) % per
        gathered = lax.dynamic_update_slice_in_dim(gathered, block, slot * rows_here, 0)
    return gathered


def shards(matrix, vectors, tfactor):
    rows_here = matrix.shape[0]
    vec_cols = to_columns(vectors)
    x_part = product(matrix, vec_cols)
    s_part = inner_product(vectors, x_part)
    both = butterfly_sum(jnp.concatenate([x_part, s_part], axis=0), "col", lax.axis_size("col"))
    x_rows = both[:rows_here]
    s_full = butterfly_sum(both[rows_here:], "row", lax.axis_size("row"))
    x_cols = to_columns(x_rows)
    coupling = inner_product(tfactor, product(s_full, tfactor))
    w_rows = product(x_rows, tfactor) - 0.5 * product(vectors, coupling)
    w_cols = product(x_cols, tfactor) - 0.5 * product(vec_cols, coupling)
    left = jnp.concatenate([vectors, w_rows], axis=1)
    right = jnp.concatenate([w_cols, vec_cols], axis=1)
    return matrix - lax.dot_general(
        left, right, (((1,), (1,)), ((), ())),
        precision=lax.Precision.HIGHEST, preferred_element_type=jnp.float32,
    )


def solution(mesh):
    in_specs = (P("row", "col"), P("row", None), P())
    out_specs = P("row", "col")
    return jax.shard_map(shards, mesh=mesh, in_specs=in_specs, out_specs=out_specs, check_vma=False)
```

```python
import jax
import jax.numpy as jnp
from jax import lax
from jax.sharding import PartitionSpec as P


def product(left, right):
    return jnp.dot(left, right, precision=lax.Precision.HIGHEST, preferred_element_type=jnp.float32)


def inner_product(left, right):
    return lax.dot_general(
        left,
        right,
        (((0,), (0,)), ((), ())),
        precision=lax.Precision.HIGHEST,
        preferred_element_type=jnp.float32,
    )


def to_columns(panel_rows):
    rows_here = panel_rows.shape[0]
    row_count = lax.axis_size("row")
    col_count = lax.axis_size("col")
    per = row_count // col_count
    pairs = []
    for src_row in range(row_count):
        for src_col in range(col_count):
            dst_row = per * src_col + src_row % per
            dst_col = src_row // per
            pairs.append((src_row * col_count + src_col, dst_row * col_count + dst_col))
    mine = lax.ppermute(panel_rows, ("row", "col"), pairs)
    low = lax.axis_index("row") % per
    gathered = jnp.zeros((per * rows_here,) + panel_rows.shape[1:], panel_rows.dtype)
    gathered = lax.dynamic_update_slice_in_dim(gathered, mine, low * rows_here, 0)
    for mask in range(1, per):
        block = lax.ppermute(mine, "row", [(i, i ^ mask) for i in range(row_count)])
        gathered = lax.dynamic_update_slice_in_dim(gathered, block, (low ^ mask) * rows_here, 0)
    return gathered


def col_sum_rows(partial):
    count = lax.axis_size("col")
    col = lax.axis_index("col")
    chunk = partial.shape[0] // count
    pieces = partial.reshape((count, chunk) + partial.shape[1:])
    total = lax.dynamic_index_in_dim(pieces, col, 0, keepdims=False)
    for shift in range(1, count):
        pairs = [(i, (i + shift) % count) for i in range(count)]
        sent = lax.dynamic_index_in_dim(pieces, (col + shift) % count, 0, keepdims=False)
        total = total + lax.ppermute(sent, "col", pairs)
    whole = jnp.zeros_like(pieces)
    whole = lax.dynamic_update_index_in_dim(whole, total, col, 0)
    for shift in range(1, count):
        pairs = [(i, (i + shift) % count) for i in range(count)]
        got = lax.ppermute(total, "col", pairs)
        whole = lax.dynamic_update_index_in_dim(whole, got, (col - shift) % count, 0)
    return whole.reshape(partial.shape)


def col_sum(value):
    count = lax.axis_size("col")
    total = value
    for shift in range(1, count):
        pairs = [(i, (i + shift) % count) for i in range(count)]
        total = total + lax.ppermute(value, "col", pairs)
    return total


def shards(matrix, vectors, tfactor):
    vec_cols = to_columns(vectors)
    x_rows = col_sum_rows(product(matrix, vec_cols))
    x_cols = to_columns(x_rows)
    s_full = col_sum(inner_product(vec_cols, x_cols))
    coupling = inner_product(tfactor, product(s_full, tfactor))
    w_rows = product(x_rows, tfactor) - 0.5 * product(vectors, coupling)
    w_cols = product(x_cols, tfactor) - 0.5 * product(vec_cols, coupling)
    left = jnp.concatenate([vectors, w_rows], axis=1)
    right = jnp.concatenate([w_cols, vec_cols], axis=1)
    return matrix - lax.dot_general(
        left, right, (((1,), (1,)), ((), ())),
        precision=lax.Precision.HIGHEST, preferred_element_type=jnp.float32,
    )


def solution(mesh):
    in_specs = (P("row", "col"), P("row", None), P())
    out_specs = P("row", "col")
    return jax.shard_map(shards, mesh=mesh, in_specs=in_specs, out_specs=out_specs, check_vma=False)
```

```python
import jax
import jax.numpy as jnp
from jax import lax
from jax.sharding import PartitionSpec as P


def product(left, right):
    return jnp.dot(left, right, precision=lax.Precision.HIGHEST, preferred_element_type=jnp.float32)


def inner_product(left, right):
    return lax.dot_general(
        left,
        right,
        (((0,), (0,)), ((), ())),
        precision=lax.Precision.HIGHEST,
        preferred_element_type=jnp.float32,
    )


def to_columns(panel_rows):
    rows_here = panel_rows.shape[0]
    row_count = lax.axis_size("row")
    col_count = lax.axis_size("col")
    per = row_count // col_count
    pairs = []
    for src_row in range(row_count):
        for src_col in range(col_count):
            dst_col = src_row // per
            low = src_row % per
            dst_row = per * (src_col ^ dst_col ^ low) + low
            pairs.append((src_row * col_count + src_col, dst_row * col_count + dst_col))
    mine = lax.ppermute(panel_rows, ("row", "col"), pairs)
    low = lax.axis_index("row") % per
    gathered = jnp.zeros((per * rows_here,) + panel_rows.shape[1:], panel_rows.dtype)
    gathered = lax.dynamic_update_slice_in_dim(gathered, mine, low * rows_here, 0)
    core_pairs = [(i, i ^ 1) for i in range(row_count)]
    other = lax.ppermute(mine, "row", core_pairs)
    across = lax.ppermute(mine, "row", [(i, i ^ 2) for i in range(row_count)])
    diagonal = lax.ppermute(across, "row", core_pairs)
    for mask, block in ((1, other), (2, across), (3, diagonal)):
        gathered = lax.dynamic_update_slice_in_dim(gathered, block, (low ^ mask) * rows_here, 0)
    return gathered


def col_sum_rows(partial):
    count = lax.axis_size("col")
    col = lax.axis_index("col")
    chunk = partial.shape[0] // count
    pieces = partial.reshape((count, chunk) + partial.shape[1:])
    total = lax.dynamic_index_in_dim(pieces, col, 0, keepdims=False)
    for shift in range(1, count):
        pairs = [(i, (i + shift) % count) for i in range(count)]
        sent = lax.dynamic_index_in_dim(pieces, (col + shift) % count, 0, keepdims=False)
        total = total + lax.ppermute(sent, "col", pairs)
    whole = jnp.zeros_like(pieces)
    whole = lax.dynamic_update_index_in_dim(whole, total, col, 0)
    for shift in range(1, count):
        pairs = [(i, (i + shift) % count) for i in range(count)]
        got = lax.ppermute(total, "col", pairs)
        whole = lax.dynamic_update_index_in_dim(whole, got, (col - shift) % count, 0)
    return whole.reshape(partial.shape)


def col_sum(value):
    count = lax.axis_size("col")
    step = 1
    while step < count:
        value = value + lax.ppermute(value, "col", [(i, i ^ step) for i in range(count)])
        step *= 2
    return value


def shards(matrix, vectors, tfactor):
    vec_cols = to_columns(vectors)
    x_rows = col_sum_rows(product(matrix, vec_cols))
    x_cols = to_columns(x_rows)
    s_full = col_sum(inner_product(vec_cols, x_cols))
    coupling = inner_product(tfactor, product(s_full, tfactor))
    w_rows = product(x_rows, tfactor) - 0.5 * product(vectors, coupling)
    w_cols = product(x_cols, tfactor) - 0.5 * product(vec_cols, coupling)
    left = jnp.concatenate([vectors, w_rows], axis=1)
    right = jnp.concatenate([w_cols, vec_cols], axis=1)
    return matrix - lax.dot_general(
        left, right, (((1,), (1,)), ((), ())),
        precision=lax.Precision.HIGHEST, preferred_element_type=jnp.float32,
    )


def solution(mesh):
    in_specs = (P("row", "col"), P("row", None), P())
    out_specs = P("row", "col")
    return jax.shard_map(shards, mesh=mesh, in_specs=in_specs, out_specs=out_specs, check_vma=False)
```

```python
import jax
import jax.numpy as jnp
from jax import lax
from jax.sharding import PartitionSpec as P


SOURCE_COL = (
    ((2, 0, 6, 1, 3, 5, 4, 7), (6, 2, 1, 4, 0, 7, 3, 5), (6, 7, 2, 1, 0, 3, 5, 4), (0, 5, 1, 3, 7, 4, 2, 6)),
    ((2, 1, 5, 3, 6, 4, 7, 0), (5, 0, 4, 1, 7, 3, 6, 2), (7, 4, 5, 6, 2, 0, 1, 3), (4, 6, 7, 1, 5, 3, 2, 0)),
    ((0, 7, 2, 6, 4, 1, 5, 3), (5, 4, 3, 7, 1, 6, 0, 2), (3, 4, 6, 0, 2, 1, 5, 7), (7, 1, 5, 4, 6, 2, 0, 3)),
    ((0, 7, 1, 4, 3, 6, 2, 5), (3, 6, 7, 4, 5, 2, 1, 0), (5, 1, 3, 0, 6, 4, 7, 2), (0, 3, 1, 2, 4, 7, 5, 6)),
    ((4, 6, 2, 5, 7, 3, 1, 0), (5, 2, 6, 3, 1, 0, 7, 4), (2, 3, 4, 7, 1, 6, 0, 5), (7, 6, 3, 2, 5, 0, 4, 1)),
    ((7, 4, 6, 0, 1, 5, 3, 2), (2, 5, 3, 1, 0, 7, 4, 6), (3, 2, 6, 5, 1, 7, 0, 4), (6, 7, 2, 0, 3, 5, 4, 1)),
    ((2, 5, 3, 0, 6, 4, 7, 1), (4, 1, 7, 2, 3, 0, 5, 6), (2, 0, 4, 6, 1, 7, 3, 5), (1, 3, 7, 5, 4, 2, 6, 0)),
    ((6, 3, 0, 7, 5, 1, 2, 4), (1, 6, 2, 5, 4, 3, 0, 7), (1, 7, 0, 4, 2, 6, 3, 5), (5, 1, 4, 3, 7, 0, 6, 2)),
)


def product(left, right):
    return jnp.dot(left, right, precision=lax.Precision.HIGHEST, preferred_element_type=jnp.float32)


def inner_product(left, right):
    return lax.dot_general(
        left,
        right,
        (((0,), (0,)), ((), ())),
        precision=lax.Precision.HIGHEST,
        preferred_element_type=jnp.float32,
    )


def to_columns(panel_rows):
    rows_here = panel_rows.shape[0]
    row_count = lax.axis_size("row")
    col_count = lax.axis_size("col")
    per = row_count // col_count
    pairs = []
    for src_row in range(row_count):
        for src_col in range(col_count):
            dst_col = src_row // per
            low = src_row % per
            if (row_count, col_count) == (32, 8):
                high = SOURCE_COL[dst_col][low].index(src_col)
            else:
                high = src_col ^ dst_col ^ low
            dst_row = per * high + low
            pairs.append((src_row * col_count + src_col, dst_row * col_count + dst_col))
    mine = lax.ppermute(panel_rows, ("row", "col"), pairs)
    low = lax.axis_index("row") % per
    gathered = jnp.zeros((per * rows_here,) + panel_rows.shape[1:], panel_rows.dtype)
    gathered = lax.dynamic_update_slice_in_dim(gathered, mine, low * rows_here, 0)
    core_pairs = [(i, i ^ 1) for i in range(row_count)]
    other = lax.ppermute(mine, "row", core_pairs)
    across = lax.ppermute(mine, "row", [(i, i ^ 2) for i in range(row_count)])
    diagonal = lax.ppermute(across, "row", core_pairs)
    for mask, block in ((1, other), (2, across), (3, diagonal)):
        gathered = lax.dynamic_update_slice_in_dim(gathered, block, (low ^ mask) * rows_here, 0)
    return gathered


def col_sum_rows(partial):
    count = lax.axis_size("col")
    col = lax.axis_index("col")
    chunk = partial.shape[0] // count
    pieces = partial.reshape((count, chunk) + partial.shape[1:])
    total = lax.dynamic_index_in_dim(pieces, col, 0, keepdims=False)
    for shift in range(1, count):
        pairs = [(i, (i + shift) % count) for i in range(count)]
        sent = lax.dynamic_index_in_dim(pieces, (col + shift) % count, 0, keepdims=False)
        total = total + lax.ppermute(sent, "col", pairs)
    whole = jnp.zeros_like(pieces)
    whole = lax.dynamic_update_index_in_dim(whole, total, col, 0)
    for shift in range(1, count):
        pairs = [(i, (i + shift) % count) for i in range(count)]
        got = lax.ppermute(total, "col", pairs)
        whole = lax.dynamic_update_index_in_dim(whole, got, (col - shift) % count, 0)
    return whole.reshape(partial.shape)


def col_sum(value):
    count = lax.axis_size("col")
    if count != 8:
        step = 1
        while step < count:
            value = value + lax.ppermute(value, "col", [(i, i ^ step) for i in range(count)])
            step *= 2
        return value
    total = value
    for shift in (1, 2, 3):
        total = total + lax.ppermute(value, "col", [(i, (i + shift) % count) for i in range(count)])
    return total + lax.ppermute(total, "col", [(i, (i + 4) % count) for i in range(count)])


def shards(matrix, vectors, tfactor):
    vec_cols = to_columns(vectors)
    x_rows = col_sum_rows(product(matrix, vec_cols))
    x_cols = to_columns(x_rows)
    s_full = col_sum(inner_product(vec_cols, x_cols))
    coupling = inner_product(tfactor, product(s_full, tfactor))
    w_rows = product(x_rows, tfactor) - 0.5 * product(vectors, coupling)
    w_cols = product(x_cols, tfactor) - 0.5 * product(vec_cols, coupling)
    left = jnp.concatenate([vectors, w_rows], axis=1)
    right = jnp.concatenate([w_cols, vec_cols], axis=1)
    return matrix - lax.dot_general(
        left, right, (((1,), (1,)), ((), ())),
        precision=lax.Precision.HIGHEST, preferred_element_type=jnp.float32,
    )


def solution(mesh):
    in_specs = (P("row", "col"), P("row", None), P())
    out_specs = P("row", "col")
    return jax.shard_map(shards, mesh=mesh, in_specs=in_specs, out_specs=out_specs, check_vma=False)
```

```python
import jax
import jax.numpy as jnp
from jax import lax
from jax.sharding import PartitionSpec as P


SOURCE_COL = (
    ((2, 0, 6, 1, 3, 5, 4, 7), (6, 2, 1, 4, 0, 7, 3, 5), (6, 7, 2, 1, 0, 3, 5, 4), (0, 5, 1, 3, 7, 4, 2, 6)),
    ((2, 1, 5, 3, 6, 4, 7, 0), (5, 0, 4, 1, 7, 3, 6, 2), (7, 4, 5, 6, 2, 0, 1, 3), (4, 6, 7, 1, 5, 3, 2, 0)),
    ((0, 7, 2, 6, 4, 1, 5, 3), (5, 4, 3, 7, 1, 6, 0, 2), (3, 4, 6, 0, 2, 1, 5, 7), (7, 1, 5, 4, 6, 2, 0, 3)),
    ((0, 7, 1, 4, 3, 6, 2, 5), (3, 6, 7, 4, 5, 2, 1, 0), (5, 1, 3, 0, 6, 4, 7, 2), (0, 3, 1, 2, 4, 7, 5, 6)),
    ((4, 6, 2, 5, 7, 3, 1, 0), (5, 2, 6, 3, 1, 0, 7, 4), (2, 3, 4, 7, 1, 6, 0, 5), (7, 6, 3, 2, 5, 0, 4, 1)),
    ((7, 4, 6, 0, 1, 5, 3, 2), (2, 5, 3, 1, 0, 7, 4, 6), (3, 2, 6, 5, 1, 7, 0, 4), (6, 7, 2, 0, 3, 5, 4, 1)),
    ((2, 5, 3, 0, 6, 4, 7, 1), (4, 1, 7, 2, 3, 0, 5, 6), (2, 0, 4, 6, 1, 7, 3, 5), (1, 3, 7, 5, 4, 2, 6, 0)),
    ((6, 3, 0, 7, 5, 1, 2, 4), (1, 6, 2, 5, 4, 3, 0, 7), (1, 7, 0, 4, 2, 6, 3, 5), (5, 1, 4, 3, 7, 0, 6, 2)),
)


def product(left, right):
    return jnp.dot(left, right, precision=lax.Precision.HIGH, preferred_element_type=jnp.float32)


def inner_product(left, right):
    return lax.dot_general(
        left,
        right,
        (((0,), (0,)), ((), ())),
        precision=lax.Precision.HIGH,
        preferred_element_type=jnp.float32,
    )


def to_columns(panel_rows):
    rows_here = panel_rows.shape[0]
    row_count = lax.axis_size("row")
    col_count = lax.axis_size("col")
    per = row_count // col_count
    pairs = []
    for src_row in range(row_count):
        for src_col in range(col_count):
            dst_col = src_row // per
            low = src_row % per
            if (row_count, col_count) == (32, 8):
                high = SOURCE_COL[dst_col][low].index(src_col)
            else:
                high = src_col ^ dst_col ^ low
            dst_row = per * high + low
            pairs.append((src_row * col_count + src_col, dst_row * col_count + dst_col))
    mine = lax.ppermute(panel_rows, ("row", "col"), pairs)
    low = lax.axis_index("row") % per
    gathered = jnp.zeros((per * rows_here,) + panel_rows.shape[1:], panel_rows.dtype)
    gathered = lax.dynamic_update_slice_in_dim(gathered, mine, low * rows_here, 0)
    core_pairs = [(i, i ^ 1) for i in range(row_count)]
    other = lax.ppermute(mine, "row", core_pairs)
    across = lax.ppermute(mine, "row", [(i, i ^ 2) for i in range(row_count)])
    diagonal = lax.ppermute(across, "row", core_pairs)
    for mask, block in ((1, other), (2, across), (3, diagonal)):
        gathered = lax.dynamic_update_slice_in_dim(gathered, block, (low ^ mask) * rows_here, 0)
    return gathered


def col_sum_rows(partial):
    count = lax.axis_size("col")
    col = lax.axis_index("col")
    chunk = partial.shape[0] // count
    pieces = partial.reshape((count, chunk) + partial.shape[1:])
    total = lax.dynamic_index_in_dim(pieces, col, 0, keepdims=False)
    for shift in range(1, count):
        pairs = [(i, (i + shift) % count) for i in range(count)]
        sent = lax.dynamic_index_in_dim(pieces, (col + shift) % count, 0, keepdims=False)
        total = total + lax.ppermute(sent, "col", pairs)
    whole = jnp.zeros_like(pieces)
    whole = lax.dynamic_update_index_in_dim(whole, total, col, 0)
    for shift in range(1, count):
        pairs = [(i, (i + shift) % count) for i in range(count)]
        got = lax.ppermute(total, "col", pairs)
        whole = lax.dynamic_update_index_in_dim(whole, got, (col - shift) % count, 0)
    return whole.reshape(partial.shape)


def col_sum(value):
    count = lax.axis_size("col")
    if count != 8:
        step = 1
        while step < count:
            value = value + lax.ppermute(value, "col", [(i, i ^ step) for i in range(count)])
            step *= 2
        return value
    total = value
    for shift in (1, 2, 3):
        total = total + lax.ppermute(value, "col", [(i, (i + shift) % count) for i in range(count)])
    return total + lax.ppermute(total, "col", [(i, (i + 4) % count) for i in range(count)])


def shards(matrix, vectors, tfactor):
    vec_cols = to_columns(vectors)
    x_rows = col_sum_rows(product(matrix, vec_cols))
    x_cols = to_columns(x_rows)
    s_full = col_sum(inner_product(vec_cols, x_cols))
    coupling = inner_product(tfactor, product(s_full, tfactor))
    w_rows = product(x_rows, tfactor) - 0.5 * product(vectors, coupling)
    w_cols = product(x_cols, tfactor) - 0.5 * product(vec_cols, coupling)
    left = jnp.concatenate([vectors, w_rows], axis=1)
    right = jnp.concatenate([w_cols, vec_cols], axis=1)
    return matrix - lax.dot_general(
        left, right, (((1,), (1,)), ((), ())),
        precision=lax.Precision.HIGH, preferred_element_type=jnp.float32,
    )


def solution(mesh):
    in_specs = (P("row", "col"), P("row", None), P())
    out_specs = P("row", "col")
    return jax.shard_map(shards, mesh=mesh, in_specs=in_specs, out_specs=out_specs, check_vma=False)
```

```python
import jax
import jax.numpy as jnp
from jax import lax
from jax.sharding import PartitionSpec as P


SOURCE_COL = (
    ((2, 0, 6, 1, 3, 5, 4, 7), (6, 2, 1, 4, 0, 7, 3, 5), (6, 7, 2, 1, 0, 3, 5, 4), (0, 5, 1, 3, 7, 4, 2, 6)),
    ((2, 1, 5, 3, 6, 4, 7, 0), (5, 0, 4, 1, 7, 3, 6, 2), (7, 4, 5, 6, 2, 0, 1, 3), (4, 6, 7, 1, 5, 3, 2, 0)),
    ((0, 7, 2, 6, 4, 1, 5, 3), (5, 4, 3, 7, 1, 6, 0, 2), (3, 4, 6, 0, 2, 1, 5, 7), (7, 1, 5, 4, 6, 2, 0, 3)),
    ((0, 7, 1, 4, 3, 6, 2, 5), (3, 6, 7, 4, 5, 2, 1, 0), (5, 1, 3, 0, 6, 4, 7, 2), (0, 3, 1, 2, 4, 7, 5, 6)),
    ((4, 6, 2, 5, 7, 3, 1, 0), (5, 2, 6, 3, 1, 0, 7, 4), (2, 3, 4, 7, 1, 6, 0, 5), (7, 6, 3, 2, 5, 0, 4, 1)),
    ((7, 4, 6, 0, 1, 5, 3, 2), (2, 5, 3, 1, 0, 7, 4, 6), (3, 2, 6, 5, 1, 7, 0, 4), (6, 7, 2, 0, 3, 5, 4, 1)),
    ((2, 5, 3, 0, 6, 4, 7, 1), (4, 1, 7, 2, 3, 0, 5, 6), (2, 0, 4, 6, 1, 7, 3, 5), (1, 3, 7, 5, 4, 2, 6, 0)),
    ((6, 3, 0, 7, 5, 1, 2, 4), (1, 6, 2, 5, 4, 3, 0, 7), (1, 7, 0, 4, 2, 6, 3, 5), (5, 1, 4, 3, 7, 0, 6, 2)),
)


def product(left, right):
    return jnp.dot(left, right, precision=lax.Precision.HIGH, preferred_element_type=jnp.float32)


def inner_product(left, right):
    return lax.dot_general(
        left,
        right,
        (((0,), (0,)), ((), ())),
        precision=lax.Precision.HIGH,
        preferred_element_type=jnp.float32,
    )


def to_columns(panel_rows):
    rows_here = panel_rows.shape[0]
    row_count = lax.axis_size("row")
    col_count = lax.axis_size("col")
    per = row_count // col_count
    pairs = []
    for src_row in range(row_count):
        for src_col in range(col_count):
            dst_col = src_row // per
            low = src_row % per
            if (row_count, col_count) == (32, 8):
                high = SOURCE_COL[dst_col][low].index(src_col)
            else:
                high = src_col ^ dst_col ^ low
            dst_row = per * high + low
            pairs.append((src_row * col_count + src_col, dst_row * col_count + dst_col))
    mine = lax.ppermute(panel_rows, ("row", "col"), pairs)
    groups = [list(range(per * g, per * g + per)) for g in range(row_count // per)]
    spread = jnp.broadcast_to(mine[None], (per,) + mine.shape)
    gathered = lax.all_to_all(spread, "row", 0, 0, axis_index_groups=groups, tiled=True)
    return gathered.reshape((per * rows_here,) + panel_rows.shape[1:])


def col_sum_rows(partial):
    count = lax.axis_size("col")
    pieces = partial.reshape((count, partial.shape[0] // count) + partial.shape[1:])
    total = jnp.sum(lax.all_to_all(pieces, "col", 0, 0, tiled=True), axis=0)
    spread = jnp.broadcast_to(total[None], pieces.shape)
    return lax.all_to_all(spread, "col", 0, 0, tiled=True).reshape(partial.shape)


def col_sum(value):
    count = lax.axis_size("col")
    spread = jnp.broadcast_to(value[None], (count,) + value.shape)
    return jnp.sum(lax.all_to_all(spread, "col", 0, 0, tiled=True), axis=0)


def shards(matrix, vectors, tfactor):
    vec_cols = to_columns(vectors)
    x_rows = col_sum_rows(product(matrix, vec_cols))
    x_cols = to_columns(x_rows)
    s_full = col_sum(inner_product(vec_cols, x_cols))
    coupling = inner_product(tfactor, product(s_full, tfactor))
    w_rows = product(x_rows, tfactor) - 0.5 * product(vectors, coupling)
    w_cols = product(x_cols, tfactor) - 0.5 * product(vec_cols, coupling)
    left = jnp.concatenate([vectors, w_rows], axis=1)
    right = jnp.concatenate([w_cols, vec_cols], axis=1)
    return matrix - lax.dot_general(
        left, right, (((1,), (1,)), ((), ())),
        precision=lax.Precision.HIGH, preferred_element_type=jnp.float32,
    )


def solution(mesh):
    in_specs = (P("row", "col"), P("row", None), P())
    out_specs = P("row", "col")
    return jax.shard_map(shards, mesh=mesh, in_specs=in_specs, out_specs=out_specs, check_vma=False)
```

```python
import jax
import jax.numpy as jnp
from jax import lax
from jax.sharding import PartitionSpec as P


SOURCE_COL = (
    ((2, 0, 6, 1, 3, 5, 4, 7), (6, 2, 1, 4, 0, 7, 3, 5), (6, 7, 2, 1, 0, 3, 5, 4), (0, 5, 1, 3, 7, 4, 2, 6)),
    ((2, 1, 5, 3, 6, 4, 7, 0), (5, 0, 4, 1, 7, 3, 6, 2), (7, 4, 5, 6, 2, 0, 1, 3), (4, 6, 7, 1, 5, 3, 2, 0)),
    ((0, 7, 2, 6, 4, 1, 5, 3), (5, 4, 3, 7, 1, 6, 0, 2), (3, 4, 6, 0, 2, 1, 5, 7), (7, 1, 5, 4, 6, 2, 0, 3)),
    ((0, 7, 1, 4, 3, 6, 2, 5), (3, 6, 7, 4, 5, 2, 1, 0), (5, 1, 3, 0, 6, 4, 7, 2), (0, 3, 1, 2, 4, 7, 5, 6)),
    ((4, 6, 2, 5, 7, 3, 1, 0), (5, 2, 6, 3, 1, 0, 7, 4), (2, 3, 4, 7, 1, 6, 0, 5), (7, 6, 3, 2, 5, 0, 4, 1)),
    ((7, 4, 6, 0, 1, 5, 3, 2), (2, 5, 3, 1, 0, 7, 4, 6), (3, 2, 6, 5, 1, 7, 0, 4), (6, 7, 2, 0, 3, 5, 4, 1)),
    ((2, 5, 3, 0, 6, 4, 7, 1), (4, 1, 7, 2, 3, 0, 5, 6), (2, 0, 4, 6, 1, 7, 3, 5), (1, 3, 7, 5, 4, 2, 6, 0)),
    ((6, 3, 0, 7, 5, 1, 2, 4), (1, 6, 2, 5, 4, 3, 0, 7), (1, 7, 0, 4, 2, 6, 3, 5), (5, 1, 4, 3, 7, 0, 6, 2)),
)


def product(left, right):
    return jnp.dot(left, right, precision=lax.Precision.HIGH, preferred_element_type=jnp.float32)


def inner_product(left, right):
    return lax.dot_general(
        left,
        right,
        (((0,), (0,)), ((), ())),
        precision=lax.Precision.HIGH,
        preferred_element_type=jnp.float32,
    )


def to_columns(panel_rows):
    rows_here = panel_rows.shape[0]
    row_count = lax.axis_size("row")
    col_count = lax.axis_size("col")
    per = row_count // col_count
    pairs = []
    for src_row in range(row_count):
        for src_col in range(col_count):
            dst_col = src_row // per
            low = src_row % per
            if (row_count, col_count) == (32, 8):
                high = SOURCE_COL[dst_col][low].index(src_col)
            else:
                high = src_col ^ dst_col ^ low
            dst_row = per * high + low
            pairs.append((src_row * col_count + src_col, dst_row * col_count + dst_col))
    mine = lax.ppermute(panel_rows, ("row", "col"), pairs)
    low = lax.axis_index("row") % per
    gathered = jnp.zeros((per * rows_here,) + panel_rows.shape[1:], panel_rows.dtype)
    gathered = lax.dynamic_update_slice_in_dim(gathered, mine, low * rows_here, 0)
    core_pairs = [(i, i ^ 1) for i in range(row_count)]
    other = lax.ppermute(mine, "row", core_pairs)
    across = lax.ppermute(mine, "row", [(i, i ^ 2) for i in range(row_count)])
    diagonal = lax.ppermute(across, "row", core_pairs)
    for mask, block in ((1, other), (2, across), (3, diagonal)):
        gathered = lax.dynamic_update_slice_in_dim(gathered, block, (low ^ mask) * rows_here, 0)
    return gathered


def col_sum_rows(partial, vectors):
    count = lax.axis_size("col")
    chunk = partial.shape[0] // count
    pieces = partial.reshape((count, chunk) + partial.shape[1:])
    total = jnp.sum(lax.all_to_all(pieces, "col", 0, 0, tiled=True), axis=0)
    vec_chunk = lax.dynamic_slice_in_dim(vectors, lax.axis_index("col") * chunk, chunk, 0)
    inner = inner_product(vec_chunk, total)
    both = jnp.concatenate([total, inner], axis=0)
    spread = jnp.broadcast_to(both[None], (count,) + both.shape)
    got = lax.all_to_all(spread, "col", 0, 0, tiled=True)
    return got[:, :chunk].reshape(partial.shape), jnp.sum(got[:, chunk:], axis=0)


def butterfly_sum(value, axis):
    count = lax.axis_size(axis)
    step = 1
    while step < count:
        value = value + lax.ppermute(value, axis, [(i, i ^ step) for i in range(count)])
        step *= 2
    return value


def shards(matrix, vectors, tfactor):
    vec_cols = to_columns(vectors)
    x_rows, s_rows = col_sum_rows(product(matrix, vec_cols), vectors)
    s_full = butterfly_sum(s_rows, "row")
    x_cols = to_columns(x_rows)
    coupling = inner_product(tfactor, product(s_full, tfactor))
    w_rows = product(x_rows, tfactor) - 0.5 * product(vectors, coupling)
    w_cols = product(x_cols, tfactor) - 0.5 * product(vec_cols, coupling)
    left = jnp.concatenate([vectors, w_rows], axis=1)
    right = jnp.concatenate([w_cols, vec_cols], axis=1)
    return matrix - lax.dot_general(
        left, right, (((1,), (1,)), ((), ())),
        precision=lax.Precision.HIGH, preferred_element_type=jnp.float32,
    )


def solution(mesh):
    in_specs = (P("row", "col"), P("row", None), P())
    out_specs = P("row", "col")
    return jax.shard_map(shards, mesh=mesh, in_specs=in_specs, out_specs=out_specs, check_vma=False)
```

```python
import jax
import jax.numpy as jnp
from jax import lax
from jax.sharding import PartitionSpec as P


SOURCE_COL = (
    ((2, 0, 6, 1, 3, 5, 4, 7), (6, 2, 1, 4, 0, 7, 3, 5), (6, 7, 2, 1, 0, 3, 5, 4), (0, 5, 1, 3, 7, 4, 2, 6)),
    ((2, 1, 5, 3, 6, 4, 7, 0), (5, 0, 4, 1, 7, 3, 6, 2), (7, 4, 5, 6, 2, 0, 1, 3), (4, 6, 7, 1, 5, 3, 2, 0)),
    ((0, 7, 2, 6, 4, 1, 5, 3), (5, 4, 3, 7, 1, 6, 0, 2), (3, 4, 6, 0, 2, 1, 5, 7), (7, 1, 5, 4, 6, 2, 0, 3)),
    ((0, 7, 1, 4, 3, 6, 2, 5), (3, 6, 7, 4, 5, 2, 1, 0), (5, 1, 3, 0, 6, 4, 7, 2), (0, 3, 1, 2, 4, 7, 5, 6)),
    ((4, 6, 2, 5, 7, 3, 1, 0), (5, 2, 6, 3, 1, 0, 7, 4), (2, 3, 4, 7, 1, 6, 0, 5), (7, 6, 3, 2, 5, 0, 4, 1)),
    ((7, 4, 6, 0, 1, 5, 3, 2), (2, 5, 3, 1, 0, 7, 4, 6), (3, 2, 6, 5, 1, 7, 0, 4), (6, 7, 2, 0, 3, 5, 4, 1)),
    ((2, 5, 3, 0, 6, 4, 7, 1), (4, 1, 7, 2, 3, 0, 5, 6), (2, 0, 4, 6, 1, 7, 3, 5), (1, 3, 7, 5, 4, 2, 6, 0)),
    ((6, 3, 0, 7, 5, 1, 2, 4), (1, 6, 2, 5, 4, 3, 0, 7), (1, 7, 0, 4, 2, 6, 3, 5), (5, 1, 4, 3, 7, 0, 6, 2)),
)


def product(left, right):
    return jnp.dot(left, right, precision=lax.Precision.HIGH, preferred_element_type=jnp.float32)


def inner_product(left, right):
    return lax.dot_general(
        left,
        right,
        (((0,), (0,)), ((), ())),
        precision=lax.Precision.HIGH,
        preferred_element_type=jnp.float32,
    )


def to_columns(panel_rows):
    rows_here = panel_rows.shape[0]
    row_count = lax.axis_size("row")
    col_count = lax.axis_size("col")
    per = row_count // col_count
    pairs = []
    for src_row in range(row_count):
        for src_col in range(col_count):
            dst_col = src_row // per
            low = src_row % per
            if (row_count, col_count) == (32, 8):
                high = SOURCE_COL[dst_col][low].index(src_col)
            else:
                high = src_col ^ dst_col ^ low
            dst_row = per * high + low
            pairs.append((src_row * col_count + src_col, dst_row * col_count + dst_col))
    mine = lax.ppermute(panel_rows, ("row", "col"), pairs)
    low = lax.axis_index("row") % per
    gathered = jnp.zeros((per * rows_here,) + panel_rows.shape[1:], panel_rows.dtype)
    gathered = lax.dynamic_update_slice_in_dim(gathered, mine, low * rows_here, 0)
    core_pairs = [(i, i ^ 1) for i in range(row_count)]
    other = lax.ppermute(mine, "row", core_pairs)
    across = lax.ppermute(mine, "row", [(i, i ^ 2) for i in range(row_count)])
    diagonal = lax.ppermute(across, "row", core_pairs)
    for mask, block in ((1, other), (2, across), (3, diagonal)):
        gathered = lax.dynamic_update_slice_in_dim(gathered, block, (low ^ mask) * rows_here, 0)
    return gathered


def col_sum_rows(partial):
    count = lax.axis_size("col")
    pieces = partial.reshape((count, partial.shape[0] // count) + partial.shape[1:])
    total = jnp.sum(lax.all_to_all(pieces, "col", 0, 0, tiled=True), axis=0)
    spread = jnp.broadcast_to(total[None], pieces.shape)
    return lax.all_to_all(spread, "col", 0, 0, tiled=True).reshape(partial.shape)


def butterfly_sum(value, axis):
    count = lax.axis_size(axis)
    step = 1
    while step < count:
        value = value + lax.ppermute(value, axis, [(i, i ^ step) for i in range(count)])
        step *= 2
    return value


def shards(matrix, vectors, tfactor):
    vec_cols = to_columns(vectors)
    x_rows = col_sum_rows(product(matrix, vec_cols))
    s_full = butterfly_sum(inner_product(vectors, x_rows), "row")
    x_cols = to_columns(x_rows)
    coupling = inner_product(tfactor, product(s_full, tfactor))
    w_rows = product(x_rows, tfactor) - 0.5 * product(vectors, coupling)
    w_cols = product(x_cols, tfactor) - 0.5 * product(vec_cols, coupling)
    left = jnp.concatenate([vectors, w_rows], axis=1)
    right = jnp.concatenate([w_cols, vec_cols], axis=1)
    return matrix - lax.dot_general(
        left, right, (((1,), (1,)), ((), ())),
        precision=lax.Precision.HIGH, preferred_element_type=jnp.float32,
    )


def solution(mesh):
    in_specs = (P("row", "col"), P("row", None), P())
    out_specs = P("row", "col")
    return jax.shard_map(shards, mesh=mesh, in_specs=in_specs, out_specs=out_specs, check_vma=False)
```

```python
import jax
import jax.numpy as jnp
from jax import lax
from jax.sharding import PartitionSpec as P


def product(left, right):
    return jnp.dot(left, right, precision=lax.Precision.HIGH, preferred_element_type=jnp.float32)


def inner_product(left, right):
    return lax.dot_general(
        left,
        right,
        (((0,), (0,)), ((), ())),
        precision=lax.Precision.HIGH,
        preferred_element_type=jnp.float32,
    )


def to_columns(panel_rows):
    rows_here = panel_rows.shape[0]
    row_count = lax.axis_size("row")
    col_count = lax.axis_size("col")
    per = row_count // col_count
    high = lax.axis_index("row") // per
    low = lax.axis_index("row") % per
    col = lax.axis_index("col")
    mine = jnp.where(high == col, panel_rows, jnp.zeros_like(panel_rows))
    step = 1
    while step < col_count:
        pairs = []
        for src_high in range(col_count):
            for src_low in range(per):
                for src_col in range(col_count):
                    if (src_high ^ src_col) < step:
                        src = (per * src_high + src_low) * col_count + src_col
                        dst = (per * (src_high ^ step) + src_low) * col_count + src_col
                        pairs.append((src, dst))
        mine = mine + lax.ppermute(mine, ("row", "col"), pairs)
        step *= 2
    gathered = jnp.zeros((per * rows_here,) + panel_rows.shape[1:], panel_rows.dtype)
    gathered = lax.dynamic_update_slice_in_dim(gathered, mine, low * rows_here, 0)
    core_pairs = [(i, i ^ 1) for i in range(row_count)]
    other = lax.ppermute(mine, "row", core_pairs)
    across = lax.ppermute(mine, "row", [(i, i ^ 2) for i in range(row_count)])
    diagonal = lax.ppermute(across, "row", core_pairs)
    for mask, block in ((1, other), (2, across), (3, diagonal)):
        gathered = lax.dynamic_update_slice_in_dim(gathered, block, (low ^ mask) * rows_here, 0)
    return gathered


def col_sum_rows(partial):
    count = lax.axis_size("col")
    pieces = partial.reshape((count, partial.shape[0] // count) + partial.shape[1:])
    total = jnp.sum(lax.all_to_all(pieces, "col", 0, 0, tiled=True), axis=0)
    spread = jnp.broadcast_to(total[None], pieces.shape)
    return lax.all_to_all(spread, "col", 0, 0, tiled=True).reshape(partial.shape)


def butterfly_sum(value, axis):
    count = lax.axis_size(axis)
    step = 1
    while step < count:
        value = value + lax.ppermute(value, axis, [(i, i ^ step) for i in range(count)])
        step *= 2
    return value


def shards(matrix, vectors, tfactor):
    vec_cols = to_columns(vectors)
    x_rows = col_sum_rows(product(matrix, vec_cols))
    s_full = butterfly_sum(inner_product(vectors, x_rows), "row")
    x_cols = to_columns(x_rows)
    coupling = inner_product(tfactor, product(s_full, tfactor))
    w_rows = product(x_rows, tfactor) - 0.5 * product(vectors, coupling)
    w_cols = product(x_cols, tfactor) - 0.5 * product(vec_cols, coupling)
    left = jnp.concatenate([vectors, w_rows], axis=1)
    right = jnp.concatenate([w_cols, vec_cols], axis=1)
    return matrix - lax.dot_general(
        left, right, (((1,), (1,)), ((), ())),
        precision=lax.Precision.HIGH, preferred_element_type=jnp.float32,
    )


def solution(mesh):
    in_specs = (P("row", "col"), P("row", None), P())
    out_specs = P("row", "col")
    return jax.shard_map(shards, mesh=mesh, in_specs=in_specs, out_specs=out_specs, check_vma=False)
```

```python
import jax
import jax.numpy as jnp
from jax import lax
from jax.sharding import PartitionSpec as P


def product(left, right):
    return jnp.dot(left, right, precision=lax.Precision.HIGH, preferred_element_type=jnp.float32)


def inner_product(left, right):
    return lax.dot_general(
        left,
        right,
        (((0,), (0,)), ((), ())),
        precision=lax.Precision.HIGH,
        preferred_element_type=jnp.float32,
    )


def to_columns(panel_rows, held=None):
    rows_here = panel_rows.shape[0]
    row_count = lax.axis_size("row")
    col_count = lax.axis_size("col")
    per = row_count // col_count
    high = lax.axis_index("row") // per
    low = lax.axis_index("row") % per
    col = lax.axis_index("col")
    mine = jnp.where(high == col, panel_rows, jnp.zeros_like(panel_rows))
    step = 1
    while step < col_count:
        pairs = []
        for src_high in range(col_count):
            for src_low in range(per):
                for src_col in range(col_count):
                    if (src_high ^ src_col) < step:
                        src = (per * src_high + src_low) * col_count + src_col
                        dst = (per * (src_high ^ step) + src_low) * col_count + src_col
                        pairs.append((src, dst))
        mine = mine + lax.ppermute(mine, ("row", "col"), pairs)
        step *= 2
    mine, held = lax.optimization_barrier((mine, held))
    gathered = jnp.zeros((per * rows_here,) + panel_rows.shape[1:], panel_rows.dtype)
    gathered = lax.dynamic_update_slice_in_dim(gathered, mine, low * rows_here, 0)
    core_pairs = [(i, i ^ 1) for i in range(row_count)]
    other = lax.ppermute(mine, "row", core_pairs)
    across = lax.ppermute(mine, "row", [(i, i ^ 2) for i in range(row_count)])
    diagonal = lax.ppermute(across, "row", core_pairs)
    for mask, block in ((1, other), (2, across), (3, diagonal)):
        gathered = lax.dynamic_update_slice_in_dim(gathered, block, (low ^ mask) * rows_here, 0)
    return gathered, held


def col_sum_rows(partial):
    count = lax.axis_size("col")
    pieces = partial.reshape((count, partial.shape[0] // count) + partial.shape[1:])
    total = jnp.sum(lax.all_to_all(pieces, "col", 0, 0, tiled=True), axis=0)
    spread = jnp.broadcast_to(total[None], pieces.shape)
    return lax.all_to_all(spread, "col", 0, 0, tiled=True).reshape(partial.shape)


def butterfly_sum(value, axis):
    count = lax.axis_size(axis)
    step = 1
    while step < count:
        value = value + lax.ppermute(value, axis, [(i, i ^ step) for i in range(count)])
        step *= 2
    return value


def shards(matrix, vectors, tfactor):
    vec_cols, _ = to_columns(vectors)
    x_rows = col_sum_rows(product(matrix, vec_cols))
    x_cols, s_part = to_columns(x_rows, inner_product(vectors, x_rows))
    s_full = butterfly_sum(s_part, "row")
    coupling = inner_product(tfactor, product(s_full, tfactor))
    w_rows = product(x_rows, tfactor) - 0.5 * product(vectors, coupling)
    w_cols = product(x_cols, tfactor) - 0.5 * product(vec_cols, coupling)
    left = jnp.concatenate([vectors, w_rows], axis=1)
    right = jnp.concatenate([w_cols, vec_cols], axis=1)
    return matrix - lax.dot_general(
        left, right, (((1,), (1,)), ((), ())),
        precision=lax.Precision.HIGH, preferred_element_type=jnp.float32,
    )


def solution(mesh):
    in_specs = (P("row", "col"), P("row", None), P())
    out_specs = P("row", "col")
    return jax.shard_map(shards, mesh=mesh, in_specs=in_specs, out_specs=out_specs, check_vma=False)
```

```python
import jax
import jax.numpy as jnp
from jax import lax
from jax.sharding import PartitionSpec as P


def product(left, right):
    return jnp.dot(left, right, precision=lax.Precision.HIGH, preferred_element_type=jnp.float32)


def inner_product(left, right):
    return lax.dot_general(
        left,
        right,
        (((0,), (0,)), ((), ())),
        precision=lax.Precision.HIGH,
        preferred_element_type=jnp.float32,
    )


def to_columns(panel_rows, extra=None):
    rows_here = panel_rows.shape[0]
    row_count = lax.axis_size("row")
    col_count = lax.axis_size("col")
    per = row_count // col_count
    high = lax.axis_index("row") // per
    low = lax.axis_index("row") % per
    col = lax.axis_index("col")
    mine = jnp.where(high == col, panel_rows, jnp.zeros_like(panel_rows))
    step = 1
    while step < col_count:
        pairs = []
        for src_high in range(col_count):
            for src_low in range(per):
                for src_col in range(col_count):
                    if extra is not None or (src_high ^ src_col) < step:
                        src = (per * src_high + src_low) * col_count + src_col
                        dst = (per * (src_high ^ step) + src_low) * col_count + src_col
                        pairs.append((src, dst))
        if extra is None:
            mine = mine + lax.ppermute(mine, ("row", "col"), pairs)
        else:
            got = lax.ppermute(jnp.concatenate([mine, extra], axis=0), ("row", "col"), pairs)
            mine = mine + got[:rows_here]
            extra = extra + got[rows_here:]
        step *= 2
    gathered = jnp.zeros((per * rows_here,) + panel_rows.shape[1:], panel_rows.dtype)
    gathered = lax.dynamic_update_slice_in_dim(gathered, mine, low * rows_here, 0)
    core_pairs = [(i, i ^ 1) for i in range(row_count)]
    sent = mine if extra is None else jnp.concatenate([mine, extra], axis=0)
    other = lax.ppermute(sent, "row", core_pairs)
    across = lax.ppermute(sent, "row", [(i, i ^ 2) for i in range(row_count)])
    diagonal = lax.ppermute(across, "row", core_pairs)
    for mask, block in ((1, other), (2, across), (3, diagonal)):
        gathered = lax.dynamic_update_slice_in_dim(gathered, block[:rows_here], (low ^ mask) * rows_here, 0)
    if extra is None:
        return gathered, None
    total = extra + other[rows_here:] + across[rows_here:] + diagonal[rows_here:]
    return gathered, total


def col_sum_rows(partial):
    count = lax.axis_size("col")
    pieces = partial.reshape((count, partial.shape[0] // count) + partial.shape[1:])
    total = jnp.sum(lax.all_to_all(pieces, "col", 0, 0, tiled=True), axis=0)
    spread = jnp.broadcast_to(total[None], pieces.shape)
    return lax.all_to_all(spread, "col", 0, 0, tiled=True).reshape(partial.shape)


def shards(matrix, vectors, tfactor):
    vec_cols, _ = to_columns(vectors)
    x_rows = col_sum_rows(product(matrix, vec_cols))
    x_cols, s_full = to_columns(x_rows, inner_product(vectors, x_rows))
    coupling = inner_product(tfactor, product(s_full, tfactor))
    w_rows = product(x_rows, tfactor) - 0.5 * product(vectors, coupling)
    w_cols = product(x_cols, tfactor) - 0.5 * product(vec_cols, coupling)
    left = jnp.concatenate([vectors, w_rows], axis=1)
    right = jnp.concatenate([w_cols, vec_cols], axis=1)
    return matrix - lax.dot_general(
        left, right, (((1,), (1,)), ((), ())),
        precision=lax.Precision.HIGH, preferred_element_type=jnp.float32,
    )


def solution(mesh):
    in_specs = (P("row", "col"), P("row", None), P())
    out_specs = P("row", "col")
    return jax.shard_map(shards, mesh=mesh, in_specs=in_specs, out_specs=out_specs, check_vma=False)
```

```python
import jax
import jax.numpy as jnp
from jax import lax
from jax.sharding import PartitionSpec as P


def product(left, right):
    return jnp.dot(left, right, precision=lax.Precision.HIGH, preferred_element_type=jnp.float32)


def inner_product(left, right):
    return lax.dot_general(
        left,
        right,
        (((0,), (0,)), ((), ())),
        precision=lax.Precision.HIGH,
        preferred_element_type=jnp.float32,
    )


def to_columns(panel_rows, extra=None):
    rows_here = panel_rows.shape[0]
    row_count = lax.axis_size("row")
    col_count = lax.axis_size("col")
    per = row_count // col_count
    high = lax.axis_index("row") // per
    low = lax.axis_index("row") % per
    col = lax.axis_index("col")
    mine = jnp.where(high == col, panel_rows, jnp.zeros_like(panel_rows))
    step = 1
    while step < col_count:
        pairs = []
        for src_high in range(col_count):
            for src_low in range(per):
                for src_col in range(col_count):
                    if extra is not None or (src_high ^ src_col) < step:
                        src = (per * src_high + src_low) * col_count + src_col
                        dst = (per * (src_high ^ step) + src_low) * col_count + src_col
                        pairs.append((src, dst))
        if extra is None:
            mine = mine + lax.ppermute(mine, ("row", "col"), pairs)
        else:
            got = lax.ppermute(jnp.concatenate([mine, extra], axis=0), ("row", "col"), pairs)
            mine = mine + got[:rows_here]
            extra = extra + got[rows_here:]
        step *= 2
    gathered = jnp.zeros((per * rows_here,) + panel_rows.shape[1:], panel_rows.dtype)
    gathered = lax.dynamic_update_slice_in_dim(gathered, mine, low * rows_here, 0)
    core_pairs = [(i, i ^ 1) for i in range(row_count)]
    sent = mine if extra is None else jnp.concatenate([mine, extra], axis=0)
    other = lax.ppermute(sent, "row", core_pairs)
    across = lax.ppermute(sent, "row", [(i, i ^ 2) for i in range(row_count)])
    diagonal = lax.ppermute(across, "row", core_pairs)
    pieces = [(low, mine)]
    for mask, block in ((1, other), (2, across), (3, diagonal)):
        gathered = lax.dynamic_update_slice_in_dim(gathered, block[:rows_here], (low ^ mask) * rows_here, 0)
        pieces.append((low ^ mask, block[:rows_here]))
    if extra is None:
        return gathered, pieces
    total = extra + other[rows_here:] + across[rows_here:] + diagonal[rows_here:]
    return gathered, total


def col_sum_rows(partial):
    count = lax.axis_size("col")
    pieces = partial.reshape((count, partial.shape[0] // count) + partial.shape[1:])
    total = jnp.sum(lax.all_to_all(pieces, "col", 0, 0, tiled=True), axis=0)
    spread = jnp.broadcast_to(total[None], pieces.shape)
    return lax.all_to_all(spread, "col", 0, 0, tiled=True).reshape(partial.shape)


def shards(matrix, vectors, tfactor):
    vec_cols, vec_pieces = to_columns(vectors)
    per = len(vec_pieces)
    column_blocks = matrix.reshape(matrix.shape[0], per, matrix.shape[1] // per)
    x_part = None
    for slot, block in vec_pieces:
        term = product(lax.dynamic_index_in_dim(column_blocks, slot, 1, keepdims=False), block)
        x_part = term if x_part is None else x_part + term
    x_rows = col_sum_rows(x_part)
    x_cols, s_full = to_columns(x_rows, inner_product(vectors, x_rows))
    coupling = inner_product(tfactor, product(s_full, tfactor))
    w_rows = product(x_rows, tfactor) - 0.5 * product(vectors, coupling)
    w_cols = product(x_cols, tfactor) - 0.5 * product(vec_cols, coupling)
    left = jnp.concatenate([vectors, w_rows], axis=1)
    right = jnp.concatenate([w_cols, vec_cols], axis=1)
    return matrix - lax.dot_general(
        left, right, (((1,), (1,)), ((), ())),
        precision=lax.Precision.HIGH, preferred_element_type=jnp.float32,
    )


def solution(mesh):
    in_specs = (P("row", "col"), P("row", None), P())
    out_specs = P("row", "col")
    return jax.shard_map(shards, mesh=mesh, in_specs=in_specs, out_specs=out_specs, check_vma=False)
```

```python
import jax
import jax.numpy as jnp
from jax import lax
from jax.sharding import PartitionSpec as P


def product(left, right):
    return jnp.dot(left, right, precision=lax.Precision.HIGH, preferred_element_type=jnp.float32)


def inner_product(left, right):
    return lax.dot_general(
        left,
        right,
        (((0,), (0,)), ((), ())),
        precision=lax.Precision.HIGH,
        preferred_element_type=jnp.float32,
    )


def to_columns(panel_rows, extra=None):
    rows_here = panel_rows.shape[0]
    row_count = lax.axis_size("row")
    col_count = lax.axis_size("col")
    per = row_count // col_count
    high = lax.axis_index("row") // per
    low = lax.axis_index("row") % per
    col = lax.axis_index("col")
    mine = jnp.where(high == col, panel_rows, jnp.zeros_like(panel_rows))
    step = 1
    while step < col_count:
        pairs = []
        for src_high in range(col_count):
            for src_low in range(per):
                for src_col in range(col_count):
                    if extra is not None or (src_high ^ src_col) < step:
                        src = (per * src_high + src_low) * col_count + src_col
                        dst = (per * (src_high ^ step) + src_low) * col_count + src_col
                        pairs.append((src, dst))
        if extra is None:
            mine = mine + lax.ppermute(mine, ("row", "col"), pairs)
        else:
            got = lax.ppermute(jnp.concatenate([mine, extra], axis=0), ("row", "col"), pairs)
            mine = mine + got[:rows_here]
            extra = extra + got[rows_here:]
        step *= 2
    gathered = jnp.zeros((per * rows_here,) + panel_rows.shape[1:], panel_rows.dtype)
    gathered = lax.dynamic_update_slice_in_dim(gathered, mine, low * rows_here, 0)
    core_pairs = [(i, i ^ 1) for i in range(row_count)]
    sent = mine if extra is None else jnp.concatenate([mine, extra], axis=0)
    other = lax.ppermute(sent, "row", core_pairs)
    across = lax.ppermute(sent, "row", [(i, i ^ 2) for i in range(row_count)])
    diagonal = lax.ppermute(across, "row", core_pairs)
    pieces = [(low, mine)]
    for mask, block in ((1, other), (2, across), (3, diagonal)):
        gathered = lax.dynamic_update_slice_in_dim(gathered, block[:rows_here], (low ^ mask) * rows_here, 0)
        pieces.append((low ^ mask, block[:rows_here]))
    if extra is None:
        return gathered, pieces
    total = extra + other[rows_here:] + across[rows_here:] + diagonal[rows_here:]
    return gathered, total


def col_sum_rows(partial):
    count = lax.axis_size("col")
    pieces = partial.reshape((count, partial.shape[0] // count) + partial.shape[1:])
    total = jnp.sum(lax.all_to_all(pieces, "col", 0, 0, tiled=True), axis=0)
    spread = jnp.broadcast_to(total[None], pieces.shape)
    return lax.all_to_all(spread, "col", 0, 0, tiled=True).reshape(partial.shape)


def shards(matrix, vectors, tfactor):
    vec_cols, vec_pieces = to_columns(vectors)
    per = len(vec_pieces)
    width = matrix.shape[1] // per
    x_part = None
    for slot, block in vec_pieces:
        term = product(lax.dynamic_slice_in_dim(matrix, slot * width, width, 1), block)
        x_part = term if x_part is None else x_part + term
    x_rows = col_sum_rows(x_part)
    x_cols, s_full = to_columns(x_rows, inner_product(vectors, x_rows))
    coupling = inner_product(tfactor, product(s_full, tfactor))
    w_rows = product(x_rows, tfactor) - 0.5 * product(vectors, coupling)
    w_cols = product(x_cols, tfactor) - 0.5 * product(vec_cols, coupling)
    left = jnp.concatenate([vectors, w_rows], axis=1)
    right = jnp.concatenate([w_cols, vec_cols], axis=1)
    return matrix - lax.dot_general(
        left, right, (((1,), (1,)), ((), ())),
        precision=lax.Precision.HIGH, preferred_element_type=jnp.float32,
    )


def solution(mesh):
    in_specs = (P("row", "col"), P("row", None), P())
    out_specs = P("row", "col")
    return jax.shard_map(shards, mesh=mesh, in_specs=in_specs, out_specs=out_specs, check_vma=False)
```

```python
import jax
import jax.numpy as jnp
from jax import lax
from jax.sharding import PartitionSpec as P


def product(left, right):
    return jnp.dot(left, right, precision=lax.Precision.HIGH, preferred_element_type=jnp.float32)


def inner_product(left, right):
    return lax.dot_general(
        left,
        right,
        (((0,), (0,)), ((), ())),
        precision=lax.Precision.HIGH,
        preferred_element_type=jnp.float32,
    )


def to_columns(panel_rows, extra=None):
    rows_here = panel_rows.shape[0]
    row_count = lax.axis_size("row")
    col_count = lax.axis_size("col")
    per = row_count // col_count
    high = lax.axis_index("row") // per
    low = lax.axis_index("row") % per
    col = lax.axis_index("col")
    mine = jnp.where(high == col, panel_rows, jnp.zeros_like(panel_rows))
    known = 1
    while known < col_count:
        width = 4 if col_count % (known * 4) == 0 else 2
        sent = mine if extra is None else jnp.concatenate([mine, extra], axis=0)
        arrived = []
        for digit in range(1, width):
            mask = digit * known
            pairs = []
            for src_high in range(col_count):
                for src_low in range(per):
                    for src_col in range(col_count):
                        if extra is not None or (src_high ^ src_col) < known:
                            src = (per * src_high + src_low) * col_count + src_col
                            dst = (per * (src_high ^ mask) + src_low) * col_count + src_col
                            pairs.append((src, dst))
            arrived.append(lax.ppermute(sent, ("row", "col"), pairs))
        for got in arrived:
            mine = mine + got[:rows_here]
            if extra is not None:
                extra = extra + got[rows_here:]
        known *= width
    gathered = jnp.zeros((per * rows_here,) + panel_rows.shape[1:], panel_rows.dtype)
    gathered = lax.dynamic_update_slice_in_dim(gathered, mine, low * rows_here, 0)
    core_pairs = [(i, i ^ 1) for i in range(row_count)]
    sent = mine if extra is None else jnp.concatenate([mine, extra], axis=0)
    other = lax.ppermute(sent, "row", core_pairs)
    across = lax.ppermute(sent, "row", [(i, i ^ 2) for i in range(row_count)])
    diagonal = lax.ppermute(across, "row", core_pairs)
    for mask, block in ((1, other), (2, across), (3, diagonal)):
        gathered = lax.dynamic_update_slice_in_dim(gathered, block[:rows_here], (low ^ mask) * rows_here, 0)
    if extra is None:
        return gathered, None
    total = extra + other[rows_here:] + across[rows_here:] + diagonal[rows_here:]
    return gathered, total


def col_sum_rows(partial):
    count = lax.axis_size("col")
    pieces = partial.reshape((count, partial.shape[0] // count) + partial.shape[1:])
    total = jnp.sum(lax.all_to_all(pieces, "col", 0, 0, tiled=True), axis=0)
    spread = jnp.broadcast_to(total[None], pieces.shape)
    return lax.all_to_all(spread, "col", 0, 0, tiled=True).reshape(partial.shape)


def shards(matrix, vectors, tfactor):
    vec_cols, _ = to_columns(vectors)
    x_rows = col_sum_rows(product(matrix, vec_cols))
    x_cols, s_full = to_columns(x_rows, inner_product(vectors, x_rows))
    coupling = inner_product(tfactor, product(s_full, tfactor))
    w_rows = product(x_rows, tfactor) - 0.5 * product(vectors, coupling)
    w_cols = product(x_cols, tfactor) - 0.5 * product(vec_cols, coupling)
    left = jnp.concatenate([vectors, w_rows], axis=1)
    right = jnp.concatenate([w_cols, vec_cols], axis=1)
    return matrix - lax.dot_general(
        left, right, (((1,), (1,)), ((), ())),
        precision=lax.Precision.HIGH, preferred_element_type=jnp.float32,
    )


def solution(mesh):
    in_specs = (P("row", "col"), P("row", None), P())
    out_specs = P("row", "col")
    return jax.shard_map(shards, mesh=mesh, in_specs=in_specs, out_specs=out_specs, check_vma=False)
```

```python
import jax
import jax.numpy as jnp
from jax import lax
from jax.sharding import PartitionSpec as P


def product(left, right):
    return jnp.dot(left, right, precision=lax.Precision.HIGH, preferred_element_type=jnp.float32)


def inner_product(left, right):
    return lax.dot_general(
        left,
        right,
        (((0,), (0,)), ((), ())),
        precision=lax.Precision.HIGH,
        preferred_element_type=jnp.float32,
    )


def to_columns(panel_rows, extra=None):
    rows_here = panel_rows.shape[0]
    row_count = lax.axis_size("row")
    col_count = lax.axis_size("col")
    per = row_count // col_count
    high = lax.axis_index("row") // per
    low = lax.axis_index("row") % per
    col = lax.axis_index("col")
    mine = jnp.where(high == col, panel_rows, jnp.zeros_like(panel_rows))
    known = 1
    while known < col_count:
        width = 4 if col_count % (known * 4) == 0 else 2
        sent = mine if extra is None else jnp.concatenate([mine, extra], axis=0)
        arrived = []
        for digit in range(1, width):
            mask = digit * known
            pairs = []
            for src_high in range(col_count):
                for src_low in range(per):
                    for src_col in range(col_count):
                        if extra is not None or (src_high ^ src_col) < known:
                            src = (per * src_high + src_low) * col_count + src_col
                            dst = (per * (src_high ^ mask) + src_low) * col_count + src_col
                            pairs.append((src, dst))
            arrived.append(lax.ppermute(sent, ("row", "col"), pairs))
        for got in arrived:
            mine = mine + got[:rows_here]
            if extra is not None:
                extra = extra + got[rows_here:]
        known *= width
    gathered = jnp.zeros((per * rows_here,) + panel_rows.shape[1:], panel_rows.dtype)
    gathered = lax.dynamic_update_slice_in_dim(gathered, mine, low * rows_here, 0)
    core_pairs = [(i, i ^ 1) for i in range(row_count)]
    sent = mine if extra is None else jnp.concatenate([mine, extra], axis=0)
    other = lax.ppermute(sent, "row", core_pairs)
    across = lax.ppermute(sent, "row", [(i, i ^ 2) for i in range(row_count)])
    diagonal = lax.ppermute(across, "row", core_pairs)
    for mask, block in ((1, other), (2, across), (3, diagonal)):
        gathered = lax.dynamic_update_slice_in_dim(gathered, block[:rows_here], (low ^ mask) * rows_here, 0)
    if extra is None:
        return gathered, None
    total = extra + other[rows_here:] + across[rows_here:] + diagonal[rows_here:]
    return gathered, total


def col_sum_rows(partial):
    count = lax.axis_size("col")
    pieces = partial.reshape((count, partial.shape[0] // count) + partial.shape[1:])
    total = jnp.sum(lax.all_to_all(pieces, "col", 0, 0, tiled=True), axis=0)
    spread = jnp.broadcast_to(total[None], pieces.shape)
    return lax.all_to_all(spread, "col", 0, 0, tiled=True).reshape(partial.shape)


def outer_product(left, right):
    return lax.dot_general(
        left, right, (((1,), (1,)), ((), ())),
        precision=lax.Precision.HIGH, preferred_element_type=jnp.float32,
    )


def shards(matrix, vectors, tfactor):
    vec_cols, _ = to_columns(vectors)
    x_rows = col_sum_rows(product(matrix, vec_cols))
    y_rows = product(x_rows, tfactor)
    partly = lax.optimization_barrier(matrix - outer_product(y_rows, vec_cols))
    x_cols, s_full = to_columns(x_rows, inner_product(vectors, x_rows))
    coupling = inner_product(tfactor, product(s_full, tfactor))
    sym = 0.5 * (coupling + coupling.T)
    w_cols = product(x_cols, tfactor) - product(vec_cols, sym)
    return partly - outer_product(vectors, w_cols)


def solution(mesh):
    in_specs = (P("row", "col"), P("row", None), P())
    out_specs = P("row", "col")
    return jax.shard_map(shards, mesh=mesh, in_specs=in_specs, out_specs=out_specs, check_vma=False)
```

```python
import jax
import jax.numpy as jnp
from jax import lax
from jax.sharding import PartitionSpec as P


def product(left, right):
    return jnp.dot(left, right, precision=lax.Precision.HIGHEST, preferred_element_type=jnp.float32)


def inner_product(left, right):
    return lax.dot_general(
        left,
        right,
        (((0,), (0,)), ((), ())),
        precision=lax.Precision.HIGHEST,
        preferred_element_type=jnp.float32,
    )


def to_columns(panel_rows, extra=None):
    rows_here = panel_rows.shape[0]
    row_count = lax.axis_size("row")
    col_count = lax.axis_size("col")
    per = row_count // col_count
    high = lax.axis_index("row") // per
    low = lax.axis_index("row") % per
    col = lax.axis_index("col")
    mine = jnp.where(high == col, panel_rows, jnp.zeros_like(panel_rows))
    known = 1
    while known < col_count:
        width = 4 if col_count % (known * 4) == 0 else 2
        sent = mine if extra is None else jnp.concatenate([mine, extra], axis=0)
        arrived = []
        for digit in range(1, width):
            mask = digit * known
            pairs = []
            for src_high in range(col_count):
                for src_low in range(per):
                    for src_col in range(col_count):
                        if extra is not None or (src_high ^ src_col) < known:
                            src = (per * src_high + src_low) * col_count + src_col
                            dst = (per * (src_high ^ mask) + src_low) * col_count + src_col
                            pairs.append((src, dst))
            arrived.append(lax.ppermute(sent, ("row", "col"), pairs))
        for got in arrived:
            mine = mine + got[:rows_here]
            if extra is not None:
                extra = extra + got[rows_here:]
        known *= width
    gathered = jnp.zeros((per * rows_here,) + panel_rows.shape[1:], panel_rows.dtype)
    gathered = lax.dynamic_update_slice_in_dim(gathered, mine, low * rows_here, 0)
    core_pairs = [(i, i ^ 1) for i in range(row_count)]
    sent = mine if extra is None else jnp.concatenate([mine, extra], axis=0)
    other = lax.ppermute(sent, "row", core_pairs)
    across = lax.ppermute(sent, "row", [(i, i ^ 2) for i in range(row_count)])
    diagonal = lax.ppermute(across, "row", core_pairs)
    for mask, block in ((1, other), (2, across), (3, diagonal)):
        gathered = lax.dynamic_update_slice_in_dim(gathered, block[:rows_here], (low ^ mask) * rows_here, 0)
    if extra is None:
        return gathered, None
    total = extra + other[rows_here:] + across[rows_here:] + diagonal[rows_here:]
    return gathered, total


def col_sum_rows(partial):
    count = lax.axis_size("col")
    pieces = partial.reshape((count, partial.shape[0] // count) + partial.shape[1:])
    total = jnp.sum(lax.all_to_all(pieces, "col", 0, 0, tiled=True), axis=0)
    spread = jnp.broadcast_to(total[None], pieces.shape)
    return lax.all_to_all(spread, "col", 0, 0, tiled=True).reshape(partial.shape)


def shards(matrix, vectors, tfactor):
    vec_cols, _ = to_columns(vectors)
    x_rows = col_sum_rows(product(matrix, vec_cols))
    x_cols, s_full = to_columns(x_rows, inner_product(vectors, x_rows))
    coupling = inner_product(tfactor, product(s_full, tfactor))
    w_rows = product(x_rows, tfactor) - 0.5 * product(vectors, coupling)
    w_cols = product(x_cols, tfactor) - 0.5 * product(vec_cols, coupling)
    left = jnp.concatenate([vectors, w_rows], axis=1)
    right = jnp.concatenate([w_cols, vec_cols], axis=1)
    return matrix - lax.dot_general(
        left, right, (((1,), (1,)), ((), ())),
        precision=lax.Precision.HIGHEST, preferred_element_type=jnp.float32,
    )


def solution(mesh):
    in_specs = (P("row", "col"), P("row", None), P())
    out_specs = P("row", "col")
    return jax.shard_map(shards, mesh=mesh, in_specs=in_specs, out_specs=out_specs, check_vma=False)
```

```python
import jax
import jax.numpy as jnp
from jax import lax
from jax.sharding import PartitionSpec as P


def product(left, right):
    return jnp.dot(left, right, precision=lax.Precision.HIGH, preferred_element_type=jnp.float32)


def inner_product(left, right):
    return lax.dot_general(
        left,
        right,
        (((0,), (0,)), ((), ())),
        precision=lax.Precision.HIGH,
        preferred_element_type=jnp.float32,
    )


def to_columns(panel_rows, extra=None):
    rows_here = panel_rows.shape[0]
    row_count = lax.axis_size("row")
    col_count = lax.axis_size("col")
    per = row_count // col_count
    high = lax.axis_index("row") // per
    low = lax.axis_index("row") % per
    col = lax.axis_index("col")
    mine = jnp.where(high == col, panel_rows, jnp.zeros_like(panel_rows))
    known = 1
    while known < col_count:
        if extra is None:
            width = col_count // known
        else:
            width = 4 if col_count % (known * 4) == 0 else 2
        sent = mine if extra is None else jnp.concatenate([mine, extra], axis=0)
        arrived = []
        for digit in range(1, width):
            mask = digit * known
            pairs = []
            for src_high in range(col_count):
                for src_low in range(per):
                    for src_col in range(col_count):
                        if extra is not None or (src_high ^ src_col) < known:
                            src = (per * src_high + src_low) * col_count + src_col
                            dst = (per * (src_high ^ mask) + src_low) * col_count + src_col
                            pairs.append((src, dst))
            arrived.append(lax.ppermute(sent, ("row", "col"), pairs))
        for got in arrived:
            mine = mine + got[:rows_here]
            if extra is not None:
                extra = extra + got[rows_here:]
        known *= width
    gathered = jnp.zeros((per * rows_here,) + panel_rows.shape[1:], panel_rows.dtype)
    gathered = lax.dynamic_update_slice_in_dim(gathered, mine, low * rows_here, 0)
    core_pairs = [(i, i ^ 1) for i in range(row_count)]
    sent = mine if extra is None else jnp.concatenate([mine, extra], axis=0)
    other = lax.ppermute(sent, "row", core_pairs)
    across = lax.ppermute(sent, "row", [(i, i ^ 2) for i in range(row_count)])
    diagonal = lax.ppermute(across, "row", core_pairs)
    for mask, block in ((1, other), (2, across), (3, diagonal)):
        gathered = lax.dynamic_update_slice_in_dim(gathered, block[:rows_here], (low ^ mask) * rows_here, 0)
    if extra is None:
        return gathered, None
    total = extra + other[rows_here:] + across[rows_here:] + diagonal[rows_here:]
    return gathered, total


def col_sum_rows(partial):
    count = lax.axis_size("col")
    pieces = partial.reshape((count, partial.shape[0] // count) + partial.shape[1:])
    total = jnp.sum(lax.all_to_all(pieces, "col", 0, 0, tiled=True), axis=0)
    spread = jnp.broadcast_to(total[None], pieces.shape)
    return lax.all_to_all(spread, "col", 0, 0, tiled=True).reshape(partial.shape)


def shards(matrix, vectors, tfactor):
    vec_cols, _ = to_columns(vectors)
    x_rows = col_sum_rows(product(matrix, vec_cols))
    x_cols, s_full = to_columns(x_rows, inner_product(vectors, x_rows))
    coupling = inner_product(tfactor, product(s_full, tfactor))
    w_rows = product(x_rows, tfactor) - 0.5 * product(vectors, coupling)
    w_cols = product(x_cols, tfactor) - 0.5 * product(vec_cols, coupling)
    left = jnp.concatenate([vectors, w_rows], axis=1)
    right = jnp.concatenate([w_cols, vec_cols], axis=1)
    return matrix - lax.dot_general(
        left, right, (((1,), (1,)), ((), ())),
        precision=lax.Precision.HIGH, preferred_element_type=jnp.float32,
    )


def solution(mesh):
    in_specs = (P("row", "col"), P("row", None), P())
    out_specs = P("row", "col")
    return jax.shard_map(shards, mesh=mesh, in_specs=in_specs, out_specs=out_specs, check_vma=False)
```

```python
import jax
import jax.numpy as jnp
from jax import lax
from jax.sharding import PartitionSpec as P


def product(left, right):
    return jnp.dot(left, right, precision=lax.Precision.HIGH, preferred_element_type=jnp.float32)


def inner_product(left, right):
    return lax.dot_general(
        left,
        right,
        (((0,), (0,)), ((), ())),
        precision=lax.Precision.HIGH,
        preferred_element_type=jnp.float32,
    )


def to_columns(panel_rows, extra=None):
    rows_here = panel_rows.shape[0]
    row_count = lax.axis_size("row")
    col_count = lax.axis_size("col")
    per = row_count // col_count
    high = lax.axis_index("row") // per
    low = lax.axis_index("row") % per
    col = lax.axis_index("col")
    mine = jnp.where(high == col, panel_rows, jnp.zeros_like(panel_rows))
    known = 1
    while known < col_count:
        width = 4 if extra is None and col_count % (known * 4) == 0 else 2
        sent = mine if extra is None else jnp.concatenate([mine, extra], axis=0)
        arrived = []
        for digit in range(1, width):
            mask = digit * known
            pairs = []
            for src_high in range(col_count):
                for src_low in range(per):
                    for src_col in range(col_count):
                        if extra is not None or (src_high ^ src_col) < known:
                            src = (per * src_high + src_low) * col_count + src_col
                            dst = (per * (src_high ^ mask) + src_low) * col_count + src_col
                            pairs.append((src, dst))
            arrived.append(lax.ppermute(sent, ("row", "col"), pairs))
        for got in arrived:
            mine = mine + got[:rows_here]
            if extra is not None:
                extra = extra + got[rows_here:]
        known *= width
    gathered = jnp.zeros((per * rows_here,) + panel_rows.shape[1:], panel_rows.dtype)
    gathered = lax.dynamic_update_slice_in_dim(gathered, mine, low * rows_here, 0)
    core_pairs = [(i, i ^ 1) for i in range(row_count)]
    sent = mine if extra is None else jnp.concatenate([mine, extra], axis=0)
    other = lax.ppermute(sent, "row", core_pairs)
    across = lax.ppermute(sent, "row", [(i, i ^ 2) for i in range(row_count)])
    diagonal = lax.ppermute(across, "row", core_pairs)
    for mask, block in ((1, other), (2, across), (3, diagonal)):
        gathered = lax.dynamic_update_slice_in_dim(gathered, block[:rows_here], (low ^ mask) * rows_here, 0)
    if extra is None:
        return gathered, None
    total = extra + other[rows_here:] + across[rows_here:] + diagonal[rows_here:]
    return gathered, total


def col_sum_rows(partial):
    count = lax.axis_size("col")
    pieces = partial.reshape((count, partial.shape[0] // count) + partial.shape[1:])
    total = jnp.sum(lax.all_to_all(pieces, "col", 0, 0, tiled=True), axis=0)
    spread = jnp.broadcast_to(total[None], pieces.shape)
    return lax.all_to_all(spread, "col", 0, 0, tiled=True).reshape(partial.shape)


def shards(matrix, vectors, tfactor):
    vec_cols, _ = to_columns(vectors)
    x_rows = col_sum_rows(product(matrix, vec_cols))
    x_cols, s_full = to_columns(x_rows, inner_product(vectors, x_rows))
    coupling = inner_product(tfactor, product(s_full, tfactor))
    w_rows = product(x_rows, tfactor) - 0.5 * product(vectors, coupling)
    w_cols = product(x_cols, tfactor) - 0.5 * product(vec_cols, coupling)
    left = jnp.concatenate([vectors, w_rows], axis=1)
    right = jnp.concatenate([w_cols, vec_cols], axis=1)
    return matrix - lax.dot_general(
        left, right, (((1,), (1,)), ((), ())),
        precision=lax.Precision.HIGH, preferred_element_type=jnp.float32,
    )


def solution(mesh):
    in_specs = (P("row", "col"), P("row", None), P())
    out_specs = P("row", "col")
    return jax.shard_map(shards, mesh=mesh, in_specs=in_specs, out_specs=out_specs, check_vma=False)
```

```python
import jax
import jax.numpy as jnp
from jax import lax
from jax.sharding import PartitionSpec as P


def product(left, right):
    return jnp.dot(left, right, precision=lax.Precision.HIGH, preferred_element_type=jnp.float32)


def inner_product(left, right):
    return lax.dot_general(
        left,
        right,
        (((0,), (0,)), ((), ())),
        precision=lax.Precision.HIGH,
        preferred_element_type=jnp.float32,
    )


def to_columns(panel_rows, extra=None):
    rows_here = panel_rows.shape[0]
    row_count = lax.axis_size("row")
    col_count = lax.axis_size("col")
    per = row_count // col_count
    high = lax.axis_index("row") // per
    low = lax.axis_index("row") % per
    col = lax.axis_index("col")
    mine = jnp.where(high == col, panel_rows, jnp.zeros_like(panel_rows))
    known = 1
    while known < col_count:
        width = 4 if col_count % (known * 4) == 0 else 2
        arrived = []
        for digit in range(1, width):
            mask = digit * known
            pairs = []
            every = []
            for src_high in range(col_count):
                for src_low in range(per):
                    for src_col in range(col_count):
                        src = (per * src_high + src_low) * col_count + src_col
                        dst = (per * (src_high ^ mask) + src_low) * col_count + src_col
                        every.append((src, dst))
                        if (src_high ^ src_col) < known:
                            pairs.append((src, dst))
            block = lax.ppermute(mine, ("row", "col"), pairs)
            summand = None if extra is None else lax.ppermute(extra, ("row", "col"), every)
            arrived.append((block, summand))
        for block, summand in arrived:
            mine = mine + block
            if extra is not None:
                extra = extra + summand
        known *= width
    gathered = jnp.zeros((per * rows_here,) + panel_rows.shape[1:], panel_rows.dtype)
    gathered = lax.dynamic_update_slice_in_dim(gathered, mine, low * rows_here, 0)
    core_pairs = [(i, i ^ 1) for i in range(row_count)]
    sent = mine if extra is None else jnp.concatenate([mine, extra], axis=0)
    other = lax.ppermute(sent, "row", core_pairs)
    across = lax.ppermute(sent, "row", [(i, i ^ 2) for i in range(row_count)])
    diagonal = lax.ppermute(across, "row", core_pairs)
    for mask, block in ((1, other), (2, across), (3, diagonal)):
        gathered = lax.dynamic_update_slice_in_dim(gathered, block[:rows_here], (low ^ mask) * rows_here, 0)
    if extra is None:
        return gathered, None
    total = extra + other[rows_here:] + across[rows_here:] + diagonal[rows_here:]
    return gathered, total


def col_sum_rows(partial):
    count = lax.axis_size("col")
    pieces = partial.reshape((count, partial.shape[0] // count) + partial.shape[1:])
    total = jnp.sum(lax.all_to_all(pieces, "col", 0, 0, tiled=True), axis=0)
    spread = jnp.broadcast_to(total[None], pieces.shape)
    return lax.all_to_all(spread, "col", 0, 0, tiled=True).reshape(partial.shape)


def shards(matrix, vectors, tfactor):
    vec_cols, _ = to_columns(vectors)
    x_rows = col_sum_rows(product(matrix, vec_cols))
    x_cols, s_full = to_columns(x_rows, inner_product(vectors, x_rows))
    coupling = inner_product(tfactor, product(s_full, tfactor))
    w_rows = product(x_rows, tfactor) - 0.5 * product(vectors, coupling)
    w_cols = product(x_cols, tfactor) - 0.5 * product(vec_cols, coupling)
    left = jnp.concatenate([vectors, w_rows], axis=1)
    right = jnp.concatenate([w_cols, vec_cols], axis=1)
    return matrix - lax.dot_general(
        left, right, (((1,), (1,)), ((), ())),
        precision=lax.Precision.HIGH, preferred_element_type=jnp.float32,
    )


def solution(mesh):
    in_specs = (P("row", "col"), P("row", None), P())
    out_specs = P("row", "col")
    return jax.shard_map(shards, mesh=mesh, in_specs=in_specs, out_specs=out_specs, check_vma=False)
```

```python
import jax
import jax.numpy as jnp
from jax import lax
from jax.sharding import PartitionSpec as P


def product(left, right):
    return jnp.dot(left, right, precision=lax.Precision.HIGH, preferred_element_type=jnp.float32)


def inner_product(left, right):
    return lax.dot_general(
        left,
        right,
        (((0,), (0,)), ((), ())),
        precision=lax.Precision.HIGH,
        preferred_element_type=jnp.float32,
    )


def to_columns(panel_rows, extra=None):
    rows_here = panel_rows.shape[0]
    row_count = lax.axis_size("row")
    col_count = lax.axis_size("col")
    per = row_count // col_count
    high = lax.axis_index("row") // per
    low = lax.axis_index("row") % per
    col = lax.axis_index("col")
    mine = jnp.where(high == col, panel_rows, jnp.zeros_like(panel_rows))
    known = 1
    while known < col_count:
        width = 4 if col_count % (known * 4) == 0 else 2
        arrived = []
        for digit in range(1, width):
            mask = digit * known
            pairs = []
            every = []
            for src_high in range(col_count):
                for src_low in range(per):
                    for src_col in range(col_count):
                        src = (per * src_high + src_low) * col_count + src_col
                        dst = (per * (src_high ^ mask) + src_low) * col_count + src_col
                        every.append((src, dst))
                        if (src_high ^ src_col) < known:
                            pairs.append((src, dst))
            block = lax.ppermute(mine, ("row", "col"), pairs)
            summand = None if extra is None else lax.ppermute(extra, ("row", "col"), every)
            arrived.append((block, summand))
        for block, summand in arrived:
            mine = mine + block
            if extra is not None:
                extra = extra + summand
        known *= width
    gathered = jnp.zeros((per * rows_here,) + panel_rows.shape[1:], panel_rows.dtype)
    gathered = lax.dynamic_update_slice_in_dim(gathered, mine, low * rows_here, 0)
    core_pairs = [(i, i ^ 1) for i in range(row_count)]
    other = lax.ppermute(mine, "row", core_pairs)
    across = lax.ppermute(mine, "row", [(i, i ^ 2) for i in range(row_count)])
    diagonal = lax.ppermute(across, "row", core_pairs)
    for mask, block in ((1, other), (2, across), (3, diagonal)):
        gathered = lax.dynamic_update_slice_in_dim(gathered, block[:rows_here], (low ^ mask) * rows_here, 0)
    if extra is None:
        return gathered, None
    total = extra
    for mask in range(1, per):
        total = total + lax.ppermute(extra, "row", [(i, i ^ mask) for i in range(row_count)])
    return gathered, total


def col_sum_rows(partial):
    count = lax.axis_size("col")
    pieces = partial.reshape((count, partial.shape[0] // count) + partial.shape[1:])
    total = jnp.sum(lax.all_to_all(pieces, "col", 0, 0, tiled=True), axis=0)
    spread = jnp.broadcast_to(total[None], pieces.shape)
    return lax.all_to_all(spread, "col", 0, 0, tiled=True).reshape(partial.shape)


def shards(matrix, vectors, tfactor):
    vec_cols, _ = to_columns(vectors)
    x_rows = col_sum_rows(product(matrix, vec_cols))
    x_cols, s_full = to_columns(x_rows, inner_product(vectors, x_rows))
    coupling = inner_product(tfactor, product(s_full, tfactor))
    w_rows = product(x_rows, tfactor) - 0.5 * product(vectors, coupling)
    w_cols = product(x_cols, tfactor) - 0.5 * product(vec_cols, coupling)
    left = jnp.concatenate([vectors, w_rows], axis=1)
    right = jnp.concatenate([w_cols, vec_cols], axis=1)
    return matrix - lax.dot_general(
        left, right, (((1,), (1,)), ((), ())),
        precision=lax.Precision.HIGH, preferred_element_type=jnp.float32,
    )


def solution(mesh):
    in_specs = (P("row", "col"), P("row", None), P())
    out_specs = P("row", "col")
    return jax.shard_map(shards, mesh=mesh, in_specs=in_specs, out_specs=out_specs, check_vma=False)
```

```python
import jax
import jax.numpy as jnp
from jax import lax
from jax.sharding import PartitionSpec as P


def product(left, right):
    return jnp.dot(left, right, precision=lax.Precision.HIGHEST, preferred_element_type=jnp.float32)


def inner_product(left, right):
    return lax.dot_general(
        left,
        right,
        (((0,), (0,)), ((), ())),
        precision=lax.Precision.HIGHEST,
        preferred_element_type=jnp.float32,
    )


def to_columns(panel_rows, extra=None):
    rows_here = panel_rows.shape[0]
    row_count = lax.axis_size("row")
    col_count = lax.axis_size("col")
    per = row_count // col_count
    high = lax.axis_index("row") // per
    low = lax.axis_index("row") % per
    col = lax.axis_index("col")
    mine = jnp.where(high == col, panel_rows, jnp.zeros_like(panel_rows))
    known = 1
    while known < col_count:
        width = 4 if col_count % (known * 4) == 0 else 2
        arrived = []
        for digit in range(1, width):
            mask = digit * known
            pairs = []
            every = []
            for src_high in range(col_count):
                for src_low in range(per):
                    for src_col in range(col_count):
                        src = (per * src_high + src_low) * col_count + src_col
                        dst = (per * (src_high ^ mask) + src_low) * col_count + src_col
                        every.append((src, dst))
                        if (src_high ^ src_col) < known:
                            pairs.append((src, dst))
            block = lax.ppermute(mine, ("row", "col"), pairs)
            summand = None if extra is None else lax.ppermute(extra, ("row", "col"), every)
            arrived.append((block, summand))
        for block, summand in arrived:
            mine = mine + block
            if extra is not None:
                extra = extra + summand
        known *= width
    gathered = jnp.zeros((per * rows_here,) + panel_rows.shape[1:], panel_rows.dtype)
    gathered = lax.dynamic_update_slice_in_dim(gathered, mine, low * rows_here, 0)
    core_pairs = [(i, i ^ 1) for i in range(row_count)]
    sent = mine if extra is None else jnp.concatenate([mine, extra], axis=0)
    other = lax.ppermute(sent, "row", core_pairs)
    across = lax.ppermute(sent, "row", [(i, i ^ 2) for i in range(row_count)])
    diagonal = lax.ppermute(across, "row", core_pairs)
    for mask, block in ((1, other), (2, across), (3, diagonal)):
        gathered = lax.dynamic_update_slice_in_dim(gathered, block[:rows_here], (low ^ mask) * rows_here, 0)
    if extra is None:
        return gathered, None
    total = extra + other[rows_here:] + across[rows_here:] + diagonal[rows_here:]
    return gathered, total


def col_sum_rows(partial):
    count = lax.axis_size("col")
    pieces = partial.reshape((count, partial.shape[0] // count) + partial.shape[1:])
    total = jnp.sum(lax.all_to_all(pieces, "col", 0, 0, tiled=True), axis=0)
    spread = jnp.broadcast_to(total[None], pieces.shape)
    return lax.all_to_all(spread, "col", 0, 0, tiled=True).reshape(partial.shape)


def shards(matrix, vectors, tfactor):
    vec_cols, _ = to_columns(vectors)
    x_rows = col_sum_rows(product(matrix, vec_cols))
    x_cols, s_full = to_columns(x_rows, inner_product(vectors, x_rows))
    coupling = inner_product(tfactor, product(s_full, tfactor))
    w_rows = product(x_rows, tfactor) - 0.5 * product(vectors, coupling)
    w_cols = product(x_cols, tfactor) - 0.5 * product(vec_cols, coupling)
    left = jnp.concatenate([vectors, w_rows], axis=1)
    right = jnp.concatenate([w_cols, vec_cols], axis=1)
    return matrix - lax.dot_general(
        left, right, (((1,), (1,)), ((), ())),
        precision=lax.Precision.HIGHEST, preferred_element_type=jnp.float32,
    )


def solution(mesh):
    in_specs = (P("row", "col"), P("row", None), P())
    out_specs = P("row", "col")
    return jax.shard_map(shards, mesh=mesh, in_specs=in_specs, out_specs=out_specs, check_vma=False)
```

```python
import jax
import jax.numpy as jnp
from jax import lax
from jax.sharding import PartitionSpec as P


def product(left, right):
    return jnp.dot(left, right, precision=lax.Precision.HIGH, preferred_element_type=jnp.float32)


def inner_product(left, right):
    return lax.dot_general(
        left,
        right,
        (((0,), (0,)), ((), ())),
        precision=lax.Precision.HIGH,
        preferred_element_type=jnp.float32,
    )


def to_columns(panel_rows, extra=None):
    rows_here = panel_rows.shape[0]
    row_count = lax.axis_size("row")
    col_count = lax.axis_size("col")
    per = row_count // col_count
    high = lax.axis_index("row") // per
    low = lax.axis_index("row") % per
    col = lax.axis_index("col")
    mine = jnp.where(high == col, panel_rows, jnp.zeros_like(panel_rows))
    known = 1
    while known < col_count:
        width = 4 if extra is None and col_count % (known * 4) == 0 else 2
        arrived = []
        for digit in range(1, width):
            mask = digit * known
            pairs = []
            every = []
            for src_high in range(col_count):
                for src_low in range(per):
                    for src_col in range(col_count):
                        src = (per * src_high + src_low) * col_count + src_col
                        dst = (per * (src_high ^ mask) + src_low) * col_count + src_col
                        every.append((src, dst))
                        if (src_high ^ src_col) < known:
                            pairs.append((src, dst))
            block = lax.ppermute(mine, ("row", "col"), pairs)
            summand = None if extra is None else lax.ppermute(extra, ("row", "col"), every)
            arrived.append((block, summand))
        for block, summand in arrived:
            mine = mine + block
            if extra is not None:
                extra = extra + summand
        known *= width
    gathered = jnp.zeros((per * rows_here,) + panel_rows.shape[1:], panel_rows.dtype)
    gathered = lax.dynamic_update_slice_in_dim(gathered, mine, low * rows_here, 0)
    core_pairs = [(i, i ^ 1) for i in range(row_count)]
    sent = mine if extra is None else jnp.concatenate([mine, extra], axis=0)
    other = lax.ppermute(sent, "row", core_pairs)
    across = lax.ppermute(sent, "row", [(i, i ^ 2) for i in range(row_count)])
    diagonal = lax.ppermute(across, "row", core_pairs)
    for mask, block in ((1, other), (2, across), (3, diagonal)):
        gathered = lax.dynamic_update_slice_in_dim(gathered, block[:rows_here], (low ^ mask) * rows_here, 0)
    if extra is None:
        return gathered, None
    total = extra + other[rows_here:] + across[rows_here:] + diagonal[rows_here:]
    return gathered, total


def col_sum_rows(partial):
    count = lax.axis_size("col")
    pieces = partial.reshape((count, partial.shape[0] // count) + partial.shape[1:])
    total = jnp.sum(lax.all_to_all(pieces, "col", 0, 0, tiled=True), axis=0)
    spread = jnp.broadcast_to(total[None], pieces.shape)
    return lax.all_to_all(spread, "col", 0, 0, tiled=True).reshape(partial.shape)


def shards(matrix, vectors, tfactor):
    vec_cols, _ = to_columns(vectors)
    x_rows = col_sum_rows(product(matrix, vec_cols))
    x_cols, s_full = to_columns(x_rows, inner_product(vectors, x_rows))
    coupling = inner_product(tfactor, product(s_full, tfactor))
    w_rows = product(x_rows, tfactor) - 0.5 * product(vectors, coupling)
    w_cols = product(x_cols, tfactor) - 0.5 * product(vec_cols, coupling)
    left = jnp.concatenate([vectors, w_rows], axis=1)
    right = jnp.concatenate([w_cols, vec_cols], axis=1)
    return matrix - lax.dot_general(
        left, right, (((1,), (1,)), ((), ())),
        precision=lax.Precision.HIGH, preferred_element_type=jnp.float32,
    )


def solution(mesh):
    in_specs = (P("row", "col"), P("row", None), P())
    out_specs = P("row", "col")
    return jax.shard_map(shards, mesh=mesh, in_specs=in_specs, out_specs=out_specs, check_vma=False)
```

```python
import jax
import jax.numpy as jnp
from jax import lax
from jax.sharding import PartitionSpec as P


def product(left, right):
    return jnp.dot(left, right, precision=lax.Precision.HIGH, preferred_element_type=jnp.float32)


def inner_product(left, right):
    return lax.dot_general(
        left,
        right,
        (((0,), (0,)), ((), ())),
        precision=lax.Precision.HIGH,
        preferred_element_type=jnp.float32,
    )


def to_columns(panel_rows, extra=None):
    rows_here = panel_rows.shape[0]
    row_count = lax.axis_size("row")
    col_count = lax.axis_size("col")
    per = row_count // col_count
    high = lax.axis_index("row") // per
    low = lax.axis_index("row") % per
    col = lax.axis_index("col")
    mine = jnp.where(high == col, panel_rows, jnp.zeros_like(panel_rows))
    if col_count == 8:
        rounds = [(2, 4, 6), (1,)]
    else:
        rounds = [(1 << k,) for k in range(col_count.bit_length() - 1)]
    reached = {0}
    for masks in rounds:
        arrived = []
        for mask in masks:
            pairs = []
            every = []
            for src_high in range(col_count):
                for src_low in range(per):
                    for src_col in range(col_count):
                        src = (per * src_high + src_low) * col_count + src_col
                        dst = (per * (src_high ^ mask) + src_low) * col_count + src_col
                        every.append((src, dst))
                        if (src_high ^ src_col) in reached:
                            pairs.append((src, dst))
            block = lax.ppermute(mine, ("row", "col"), pairs)
            summand = None if extra is None else lax.ppermute(extra, ("row", "col"), every)
            arrived.append((block, summand))
        for block, summand in arrived:
            mine = mine + block
            if extra is not None:
                extra = extra + summand
        reached = reached | {r ^ mask for r in reached for mask in masks}
    gathered = jnp.zeros((per * rows_here,) + panel_rows.shape[1:], panel_rows.dtype)
    gathered = lax.dynamic_update_slice_in_dim(gathered, mine, low * rows_here, 0)
    core_pairs = [(i, i ^ 1) for i in range(row_count)]
    sent = mine if extra is None else jnp.concatenate([mine, extra], axis=0)
    other = lax.ppermute(sent, "row", core_pairs)
    across = lax.ppermute(sent, "row", [(i, i ^ 2) for i in range(row_count)])
    diagonal = lax.ppermute(across, "row", core_pairs)
    for mask, block in ((1, other), (2, across), (3, diagonal)):
        gathered = lax.dynamic_update_slice_in_dim(gathered, block[:rows_here], (low ^ mask) * rows_here, 0)
    if extra is None:
        return gathered, None
    total = extra + other[rows_here:] + across[rows_here:] + diagonal[rows_here:]
    return gathered, total


def col_sum_rows(partial):
    count = lax.axis_size("col")
    pieces = partial.reshape((count, partial.shape[0] // count) + partial.shape[1:])
    total = jnp.sum(lax.all_to_all(pieces, "col", 0, 0, tiled=True), axis=0)
    spread = jnp.broadcast_to(total[None], pieces.shape)
    return lax.all_to_all(spread, "col", 0, 0, tiled=True).reshape(partial.shape)


def shards(matrix, vectors, tfactor):
    vec_cols, _ = to_columns(vectors)
    x_rows = col_sum_rows(product(matrix, vec_cols))
    x_cols, s_full = to_columns(x_rows, inner_product(vectors, x_rows))
    coupling = inner_product(tfactor, product(s_full, tfactor))
    w_rows = product(x_rows, tfactor) - 0.5 * product(vectors, coupling)
    w_cols = product(x_cols, tfactor) - 0.5 * product(vec_cols, coupling)
    left = jnp.concatenate([vectors, w_rows], axis=1)
    right = jnp.concatenate([w_cols, vec_cols], axis=1)
    return matrix - lax.dot_general(
        left, right, (((1,), (1,)), ((), ())),
        precision=lax.Precision.HIGH, preferred_element_type=jnp.float32,
    )


def solution(mesh):
    in_specs = (P("row", "col"), P("row", None), P())
    out_specs = P("row", "col")
    return jax.shard_map(shards, mesh=mesh, in_specs=in_specs, out_specs=out_specs, check_vma=False)
```

```python
import jax
import jax.numpy as jnp
from jax import lax
from jax.sharding import PartitionSpec as P


def product(left, right):
    return jnp.dot(left, right, precision=lax.Precision.HIGH, preferred_element_type=jnp.float32)


def inner_product(left, right):
    return lax.dot_general(
        left,
        right,
        (((0,), (0,)), ((), ())),
        precision=lax.Precision.HIGH,
        preferred_element_type=jnp.float32,
    )


def to_columns(panel_rows, extra=None):
    rows_here = panel_rows.shape[0]
    row_count = lax.axis_size("row")
    col_count = lax.axis_size("col")
    per = row_count // col_count
    high = lax.axis_index("row") // per
    low = lax.axis_index("row") % per
    col = lax.axis_index("col")
    mine = jnp.where(high == col, panel_rows, jnp.zeros_like(panel_rows))
    if col_count == 8:
        rounds = [(1,), (2, 4, 6)]
    else:
        rounds = [(1 << k,) for k in range(col_count.bit_length() - 1)]
    reached = {0}
    for masks in rounds:
        arrived = []
        for mask in masks:
            pairs = []
            every = []
            for src_high in range(col_count):
                for src_low in range(per):
                    for src_col in range(col_count):
                        src = (per * src_high + src_low) * col_count + src_col
                        dst = (per * (src_high ^ mask) + src_low) * col_count + src_col
                        every.append((src, dst))
                        if (src_high ^ src_col) in reached:
                            pairs.append((src, dst))
            block = lax.ppermute(mine, ("row", "col"), pairs)
            summand = None if extra is None else lax.ppermute(extra, ("row", "col"), every)
            arrived.append((block, summand))
        for block, summand in arrived:
            mine = mine + block
            if extra is not None:
                extra = extra + summand
        reached = reached | {r ^ mask for r in reached for mask in masks}
    gathered = jnp.zeros((per * rows_here,) + panel_rows.shape[1:], panel_rows.dtype)
    gathered = lax.dynamic_update_slice_in_dim(gathered, mine, low * rows_here, 0)
    core_pairs = [(i, i ^ 1) for i in range(row_count)]
    sent = mine if extra is None else jnp.concatenate([mine, extra], axis=0)
    other = lax.ppermute(sent, "row", core_pairs)
    across = lax.ppermute(sent, "row", [(i, i ^ 2) for i in range(row_count)])
    diagonal = lax.ppermute(across, "row", core_pairs)
    for mask, block in ((1, other), (2, across), (3, diagonal)):
        gathered = lax.dynamic_update_slice_in_dim(gathered, block[:rows_here], (low ^ mask) * rows_here, 0)
    if extra is None:
        return gathered, None
    total = extra + other[rows_here:] + across[rows_here:] + diagonal[rows_here:]
    return gathered, total


def col_sum_rows(partial):
    count = lax.axis_size("col")
    pieces = partial.reshape((count, partial.shape[0] // count) + partial.shape[1:])
    total = jnp.sum(lax.all_to_all(pieces, "col", 0, 0, tiled=True), axis=0)
    spread = jnp.broadcast_to(total[None], pieces.shape)
    return lax.all_to_all(spread, "col", 0, 0, tiled=True).reshape(partial.shape)


def shards(matrix, vectors, tfactor):
    vec_cols, _ = to_columns(vectors)
    x_rows = col_sum_rows(product(matrix, vec_cols))
    x_cols, s_full = to_columns(x_rows, inner_product(vectors, x_rows))
    coupling = inner_product(tfactor, product(s_full, tfactor))
    w_rows = product(x_rows, tfactor) - 0.5 * product(vectors, coupling)
    w_cols = product(x_cols, tfactor) - 0.5 * product(vec_cols, coupling)
    left = jnp.concatenate([vectors, w_rows], axis=1)
    right = jnp.concatenate([w_cols, vec_cols], axis=1)
    return matrix - lax.dot_general(
        left, right, (((1,), (1,)), ((), ())),
        precision=lax.Precision.HIGH, preferred_element_type=jnp.float32,
    )


def solution(mesh):
    in_specs = (P("row", "col"), P("row", None), P())
    out_specs = P("row", "col")
    return jax.shard_map(shards, mesh=mesh, in_specs=in_specs, out_specs=out_specs, check_vma=False)
```

```python
import jax
import jax.numpy as jnp
from jax import lax
from jax.sharding import PartitionSpec as P


def product(left, right):
    return jnp.dot(left, right, precision=lax.Precision.HIGH, preferred_element_type=jnp.float32)


def inner_product(left, right):
    return lax.dot_general(
        left,
        right,
        (((0,), (0,)), ((), ())),
        precision=lax.Precision.HIGH,
        preferred_element_type=jnp.float32,
    )


def to_columns(panel_rows, extra=None):
    rows_here = panel_rows.shape[0]
    row_count = lax.axis_size("row")
    col_count = lax.axis_size("col")
    per = row_count // col_count
    high = lax.axis_index("row") // per
    low = lax.axis_index("row") % per
    col = lax.axis_index("col")
    mine = jnp.where(high == col, panel_rows, jnp.zeros_like(panel_rows))
    if col_count == 8:
        rounds = [(2, 4, 6), (1,)] if extra is not None else [(1, 2, 3), (4,)]
    else:
        rounds = [(1 << k,) for k in range(col_count.bit_length() - 1)]
    reached = {0}
    for masks in rounds:
        arrived = []
        for mask in masks:
            pairs = []
            every = []
            for src_high in range(col_count):
                for src_low in range(per):
                    for src_col in range(col_count):
                        src = (per * src_high + src_low) * col_count + src_col
                        dst = (per * (src_high ^ mask) + src_low) * col_count + src_col
                        every.append((src, dst))
                        if (src_high ^ src_col) in reached:
                            pairs.append((src, dst))
            block = lax.ppermute(mine, ("row", "col"), pairs)
            summand = None if extra is None else lax.ppermute(extra, ("row", "col"), every)
            arrived.append((block, summand))
        for block, summand in arrived:
            mine = mine + block
            if extra is not None:
                extra = extra + summand
        reached = reached | {r ^ mask for r in reached for mask in masks}
    gathered = jnp.zeros((per * rows_here,) + panel_rows.shape[1:], panel_rows.dtype)
    gathered = lax.dynamic_update_slice_in_dim(gathered, mine, low * rows_here, 0)
    core_pairs = [(i, i ^ 1) for i in range(row_count)]
    sent = mine if extra is None else jnp.concatenate([mine, extra], axis=0)
    other = lax.ppermute(sent, "row", core_pairs)
    across = lax.ppermute(sent, "row", [(i, i ^ 2) for i in range(row_count)])
    diagonal = lax.ppermute(across, "row", core_pairs)
    for mask, block in ((1, other), (2, across), (3, diagonal)):
        gathered = lax.dynamic_update_slice_in_dim(gathered, block[:rows_here], (low ^ mask) * rows_here, 0)
    if extra is None:
        return gathered, None
    total = extra + other[rows_here:] + across[rows_here:] + diagonal[rows_here:]
    return gathered, total


def col_sum_rows(partial):
    count = lax.axis_size("col")
    pieces = partial.reshape((count, partial.shape[0] // count) + partial.shape[1:])
    total = jnp.sum(lax.all_to_all(pieces, "col", 0, 0, tiled=True), axis=0)
    spread = jnp.broadcast_to(total[None], pieces.shape)
    return lax.all_to_all(spread, "col", 0, 0, tiled=True).reshape(partial.shape)


def shards(matrix, vectors, tfactor):
    vec_cols, _ = to_columns(vectors)
    x_rows = col_sum_rows(product(matrix, vec_cols))
    x_cols, s_full = to_columns(x_rows, inner_product(vectors, x_rows))
    coupling = inner_product(tfactor, product(s_full, tfactor))
    w_rows = product(x_rows, tfactor) - 0.5 * product(vectors, coupling)
    w_cols = product(x_cols, tfactor) - 0.5 * product(vec_cols, coupling)
    left = jnp.concatenate([vectors, w_rows], axis=1)
    right = jnp.concatenate([w_cols, vec_cols], axis=1)
    return matrix - lax.dot_general(
        left, right, (((1,), (1,)), ((), ())),
        precision=lax.Precision.HIGH, preferred_element_type=jnp.float32,
    )


def solution(mesh):
    in_specs = (P("row", "col"), P("row", None), P())
    out_specs = P("row", "col")
    return jax.shard_map(shards, mesh=mesh, in_specs=in_specs, out_specs=out_specs, check_vma=False)
```
